768 devices in a mesh: blk: 24 (over x, z_hi, core), heads: 32 (over z_lo, y).
Axes of the slice: x: 4, y: 8, z: 12 (z_hi: 3, z_lo: 4; z = z_hi * 4 + z_lo), core: 2. Of those that a mesh axis runs over, the one named last changes fastest.
Arguments:
- q_nope: bfloat16 [3072, 8192], P('blk', 'heads'), may hold values from -6 to 6
- q_rope: bfloat16 [3072, 4096], P('blk', 'heads'), may hold values from -60 to 60
- d_out: bfloat16 [3072, 8192], P('blk', 'heads'), may hold values from -6 to 6
- latent: bfloat16 [3072, 576], P('blk'), may hold values from -6 to 6
- scale_exp: int32 [4, 3072], P(None, 'blk'), may hold values from -1 to 1
- positions: int32 [3072], P('blk'), may hold values from 0 to 3071, as said below
- spans: int32 [3072], P('blk'), may hold values from 0 to 3071
- w_uk: bfloat16 [512, 8192], P(None, 'heads'), may hold values from -0.25 to 0.25
- w_uv: bfloat16 [512, 8192], P(None, 'heads'), may hold values from -0.25 to 0.25
Outputs:
- grad_q_nope: bfloat16 [3072, 8192], P('blk', 'heads')
- grad_q_rope: bfloat16 [3072, 4096], P('blk', 'heads')
- grad_latent: bfloat16 [3072, 512], P('blk')
- grad_w_uk: float32 [512, 8192], P(None, 'heads')
- grad_w_uv: float32 [512, 8192], P(None, 'heads')
The draws below stay inside these ranges and needn't reach their ends.
Inputs may be any that keep to these rules, and one draw needn't show every extreme that they name: A permutation of the positions that maps each aligned run of 64 rows onto 64 consecutive positions in order.
All inputs are finite; a program needn't handle non-finite values.
Results may differ from the reference program's by a relative error of at most 0.02.
Values may be sent and summed in bfloat16 or wider, within the bound.
No kernel may reach another device: no remote copies, remote signals or barrier semaphores. Data moves between devices by JAX's collectives and lax.ppermute only.
A program may use at most 32 MiB of HBM per device.

```python
import jax
import jax.numpy as jnp
from jax import lax

D_LAT = 512
D_ROPE = 64
D_NOPE = 128
D_V = 128
LAT_GROUPS = 4
PB = 64
TOK_DEV = 128
HEADS = 64
TOKENS = 3072
N_BLK = 24


def draw_latent(key, part):
    own_key = jax.random.fold_in(key, 11)
    shape_all = (TOKENS, D_LAT + D_ROPE)
    drawn = jnp.clip(jax.random.normal(own_key, shape_all, jnp.float32), -6.0, 6.0)
    return drawn.astype(jnp.bfloat16)


def draw_q_rope(key, part):
    own_key = jax.random.fold_in(key, 23)
    shape_all = (TOKENS, HEADS * D_ROPE)
    drawn = jnp.clip(jax.random.normal(own_key, shape_all, jnp.float32), -6.0, 6.0)
    return drawn.astype(jnp.bfloat16)


def draw_positions(key, part):
    run_count = TOKENS // PB
    order = jax.random.permutation(jax.random.fold_in(key, 37), run_count)
    token_index = jnp.arange(TOKENS, dtype=jnp.int32)
    return (order[token_index // PB] * PB + token_index % PB).astype(jnp.int32)


def with_ends(values, key, least, high):
    index_at = [jax.random.randint(jax.random.fold_in(key, axis), (), 0, length) for axis, length in enumerate(values.shape)]
    longest = values.shape.index(max(values.shape))
    neighbour = index_at[:longest] + [(index_at[longest] + 1) % values.shape[longest]] + index_at[longest + 1:]
    return values.at[tuple(index_at)].set(least).at[tuple(neighbour)].set(high)


def levels(key, dims, pieces, smallest, high):
    level = 1.0
    for axis_at, blocks in pieces:
        draws = jax.random.uniform(jax.random.fold_in(jax.random.fold_in(key, 6), axis_at), (blocks,), jnp.float32, smallest / len(pieces), high / len(pieces))
        level = level * jnp.repeat(jnp.exp(draws), dims[axis_at] // blocks).reshape((-1,) + (1,) * (len(dims) - 1 - axis_at))
    return level


def scatter_about(key, dims, scale, bound, cuts=(), kind=jnp.bfloat16):
    result = jax.random.normal(key, dims, jnp.float32) * scale
    if len(cuts) > 0:
        result = levels(key, dims, cuts, -0.22, 0.18) * result
    return jnp.clip(result, min=-bound, max=bound).astype(kind)


def setup_inputs(seed: int = 0) -> dict:
    splits = jax.random.split(jax.random.key(seed), 10)
    return {
        "q_nope": scatter_about(splits[0], (TOKENS, HEADS * D_NOPE), 1.0, 6.0, ((0, 24), (1, 32))),
        "q_rope": draw_q_rope(jax.random.fold_in(splits[9], 71), 0),
        "d_out": scatter_about(splits[2], (TOKENS, HEADS * D_V), 1.0, 6.0, ((0, 24), (1, 32))),
        "latent": draw_latent(jax.random.fold_in(splits[9], 71), 0),
        "scale_exp": with_ends(jax.random.randint(splits[4], (LAT_GROUPS, TOKENS), -1, 2), jax.random.fold_in(splits[4], 1), -1, 1).astype(jnp.int32),
        "positions": draw_positions(jax.random.fold_in(splits[9], 71), 0),
        "spans": with_ends(jax.random.randint(splits[6], (TOKENS,), 0, TOKENS), jax.random.fold_in(splits[6], 1), 0, TOKENS - 1).astype(jnp.int32),
        "w_uk": scatter_about(splits[7], (D_LAT, HEADS * D_NOPE), D_LAT ** -0.5, 0.25, ((1, 32),)),
        "w_uv": scatter_about(splits[8], (D_LAT, HEADS * D_V), D_LAT ** -0.5, 0.25, ((1, 32),)),
    }


lowest = -1.0e30
highest = lax.Precision.HIGHEST


def rounded(values_in):
    return lax.optimization_barrier(values_in.astype(jnp.bfloat16)).astype(jnp.float32)


def reference(q_nope, q_rope, d_out, latent, scale_exp, positions, spans, w_uk, w_uv):
    token_count = q_nope.shape[0]
    head_count = w_uk.shape[1] // D_NOPE
    col_group = D_LAT // LAT_GROUPS
    factor = jnp.exp2(jnp.repeat(jnp.transpose(scale_exp), col_group, axis=1).astype(jnp.float32))
    compressed = (latent[:, :D_LAT].astype(jnp.float32) * factor).astype(jnp.bfloat16)
    key_rope = latent[:, D_LAT:].astype(jnp.float32)
    key_all = jnp.dot(compressed, w_uk, preferred_element_type=jnp.float32).astype(jnp.bfloat16)
    value_all = jnp.dot(compressed, w_uv, preferred_element_type=jnp.float32).astype(jnp.bfloat16)
    visible = (positions[None, :] <= positions[:, None]) & (positions[None, :] >= positions[:, None] - spans[:, None])
    soft_scale = (D_NOPE + D_ROPE) ** -0.5

    def by_head(matrix, width_head):
        return jnp.transpose(matrix.reshape(token_count, head_count, width_head), (1, 0, 2))

    def per_head(head_stack):
        query_n, query_r, grad_o, key_n, value_n = [member.astype(jnp.float32) for member in head_stack]
        scores = (jnp.dot(query_n, key_n.T, precision=highest) + jnp.dot(query_r, key_rope.T, precision=highest)) * soft_scale
        masked = jnp.where(visible, scores, lowest)
        row_max = jnp.max(masked, axis=1, keepdims=True)
        row_sum = jnp.sum(jnp.where(visible, jnp.exp(masked - row_max), 0.0), axis=1, keepdims=True)
        log_norm = row_max + jnp.log(row_sum)
        prob_float = jnp.where(visible, jnp.exp(scores - log_norm), 0.0)
        grad_prob = jnp.dot(grad_o, value_n.T, precision=highest)
        delta_rows = jnp.sum(prob_float * grad_prob, axis=1, keepdims=True)
        grad_score = rounded(prob_float * (grad_prob - delta_rows) * soft_scale)
        prob_half = rounded(prob_float)
        return (jnp.dot(grad_score, key_n, precision=highest),
                jnp.dot(grad_score, key_rope, precision=highest),
                jnp.dot(grad_score.T, query_n, precision=highest),
                jnp.dot(prob_half.T, grad_o, precision=highest))

    head_stack = (by_head(q_nope, D_NOPE), by_head(q_rope, D_ROPE), by_head(d_out, D_V),
                  by_head(key_all, D_NOPE), by_head(value_all, D_V))
    query_grad, rope_grad, key_grad, value_grad = lax.map(per_head, head_stack)

    def flat(stacked):
        return jnp.transpose(stacked, (1, 0, 2)).reshape(token_count, -1)

    grad_q_nope = flat(query_grad).astype(jnp.bfloat16)
    grad_q_rope = flat(rope_grad).astype(jnp.bfloat16)
    key_flat = flat(key_grad).astype(jnp.bfloat16)
    value_flat = flat(value_grad).astype(jnp.bfloat16)
    latent_sum = jnp.dot(key_flat, w_uk.T, preferred_element_type=jnp.float32) + jnp.dot(value_flat, w_uv.T, preferred_element_type=jnp.float32)
    grad_latent = (latent_sum * factor).astype(jnp.bfloat16)

    def add_shard(running, shard_rows):
        block_latent, block_key, block_value = shard_rows
        part_key = rounded(jnp.dot(block_latent.T, block_key, preferred_element_type=jnp.float32))
        part_value = rounded(jnp.dot(block_latent.T, block_value, preferred_element_type=jnp.float32))
        return (running[0] + part_key, running[1] + part_value), None

    start_sums = (jnp.zeros((D_LAT, head_count * D_NOPE), jnp.float32), jnp.zeros((D_LAT, head_count * D_V), jnp.float32))
    shards = (compressed.reshape(N_BLK, TOK_DEV, D_LAT), key_flat.reshape(N_BLK, TOK_DEV, -1), value_flat.reshape(N_BLK, TOK_DEV, -1))
    weight_sums, unused = lax.scan(add_shard, start_sums, shards)
    return (grad_q_nope, grad_q_rope, grad_latent, weight_sums[0], weight_sums[1])
```

```python
import jax
import jax.numpy as jnp
from jax import lax
from jax.sharding import PartitionSpec as P

D_ROPE = 64
D_NOPE = 128
D_V = 128
POS_SPLIT = 64
W_CHUNK = 6


lowest = -1e30


def digits_of(size):
    found = []
    stride = 1
    rest = size
    for prime in (2, 3):
        if rest % prime == 0:
            found.append((prime, stride))
            stride *= prime
            rest //= prime
    prime = 2
    while rest > 1:
        while rest % prime == 0:
            found.append((prime, stride))
            stride *= prime
            rest //= prime
        prime += 1
    return found


def gather_order(size):
    found = digits_of(size)
    odd = [d for d in found if d[0] != 2]
    even = sorted([d for d in found if d[0] == 2], key=lambda d: -d[1])
    return odd + even


def digit_value(axis, radix, stride):
    return (lax.axis_index(axis) // stride) % radix


def shift_digit(x, axis, radix, stride, by):
    size = lax.axis_size(axis)
    pairs = []
    for i in range(size):
        r = (i // stride) % radix
        pairs.append((i, i + (((r + by) % radix) - r) * stride))
    return lax.ppermute(x, axis, pairs)


def ordered_pieces(own, axis, radix, stride):
    r = digit_value(axis, radix, stride)
    received = {by: shift_digit(own, axis, radix, stride, by) for by in range(1, radix)}
    pieces = []
    for k in range(radix):
        piece = own
        for by in range(1, radix):
            piece = jnp.where((r - k) % radix == by, received[by], piece)
        pieces.append(piece)
    return pieces


def gather_blocks(block, axis):
    size = lax.axis_size(axis)
    done = []
    buf = block
    for radix, stride in gather_order(size):
        pieces = ordered_pieces(buf, axis, radix, stride)
        at = sum(1 for unused, other in done if other > stride)
        buf = jnp.stack(pieces, axis=at)
        done.append((radix, stride))
    return buf.reshape((size,) + block.shape)


def scatter_sum(data, axis):
    size = lax.axis_size(axis)
    canon = sorted(digits_of(size), key=lambda d: -d[1])
    data = data.reshape(tuple(d[0] for d in canon) + data.shape[1:])
    remaining = list(canon)
    for radix, stride in reversed(gather_order(size)):
        at = remaining.index((radix, stride))
        r = digit_value(axis, radix, stride)
        total = lax.dynamic_index_in_dim(data, r, at, keepdims=False)
        for by in range(1, radix):
            part = lax.dynamic_index_in_dim(data, (r + by) % radix, at, keepdims=False)
            total = total + shift_digit(part, axis, radix, stride, by)
        data = total
        remaining.pop(at)
    return data


def total_over(x, axis):
    size = lax.axis_size(axis)
    for radix, stride in digits_of(size):
        if radix == 2:
            x = x + shift_digit(x, axis, radix, stride, 1)
        else:
            pieces = ordered_pieces(x, axis, radix, stride)
            x = pieces[0]
            for piece in pieces[1:]:
                x = x + piece
    return x


def body(q_nope, q_rope, d_out, latent, scale_exp, positions, spans, w_uk, w_uv):
    row_count = q_nope.shape[0]
    head_count = w_uk.shape[1] // D_NOPE
    col_width = latent.shape[1] - D_ROPE
    col_group = col_width // scale_exp.shape[0]
    block_count = lax.axis_size("blk")
    key_count = row_count * block_count
    soft_scale = (D_NOPE + D_ROPE) ** (-0.5)

    factor = jnp.exp2(jnp.repeat(jnp.transpose(scale_exp), col_group, axis=1).astype(jnp.float32))
    compressed = (latent[:, :col_width].astype(jnp.float32) * factor).astype(jnp.bfloat16)
    pos_hi = (positions // POS_SPLIT).astype(jnp.bfloat16)
    pos_lo = (positions % POS_SPLIT).astype(jnp.bfloat16)
    packed = jnp.concatenate(
        [compressed, latent[:, col_width:], pos_hi[:, None], pos_lo[:, None]], axis=1
    )
    everything = gather_blocks(packed, "blk").reshape(key_count, packed.shape[1])
    comp_all = everything[:, :col_width]
    rope_all = everything[:, col_width : col_width + D_ROPE]
    key_pos = everything[:, col_width + D_ROPE].astype(jnp.int32) * POS_SPLIT + everything[
        :, col_width + D_ROPE + 1
    ].astype(jnp.int32)

    keys = jnp.dot(comp_all, w_uk, preferred_element_type=jnp.float32).astype(jnp.bfloat16)
    values = jnp.dot(comp_all, w_uv, preferred_element_type=jnp.float32).astype(jnp.bfloat16)
    keys = keys.reshape(key_count, head_count, D_NOPE)
    values = values.reshape(key_count, head_count, D_V)
    queries = q_nope.reshape(row_count, head_count, D_NOPE)
    query_rope = q_rope.reshape(row_count, head_count, D_ROPE)
    grad_out = d_out.reshape(row_count, head_count, D_V)

    scores = jnp.einsum("qhd,khd->hqk", queries, keys, preferred_element_type=jnp.float32)
    scores = scores + jnp.einsum(
        "qhr,kr->hqk", query_rope, rope_all, preferred_element_type=jnp.float32
    )
    scores = scores * soft_scale
    pairs = (key_pos[None, :] <= positions[:, None]) & (
        key_pos[None, :] >= positions[:, None] - spans[:, None]
    )
    masked = jnp.where(pairs[None], scores, lowest)
    row_max = jnp.max(masked, axis=2, keepdims=True)
    row_sum = jnp.sum(
        jnp.where(pairs[None], jnp.exp(masked - row_max), 0.0), axis=2, keepdims=True
    )
    log_norm = row_max + jnp.log(row_sum)
    prob_float = jnp.where(pairs[None], jnp.exp(scores - log_norm), 0.0)
    grad_prob = jnp.einsum("qhd,khd->hqk", grad_out, values, preferred_element_type=jnp.float32)
    delta_rows = jnp.sum(prob_float * grad_prob, axis=2, keepdims=True)
    grad_score = (prob_float * (grad_prob - delta_rows) * soft_scale).astype(jnp.bfloat16)
    prob_half = prob_float.astype(jnp.bfloat16)

    query_grad = jnp.einsum("hqk,khd->qhd", grad_score, keys, preferred_element_type=jnp.float32)
    rope_grad = jnp.einsum("hqk,kr->qhr", grad_score, rope_all, preferred_element_type=jnp.float32)
    key_grad = jnp.einsum("hqk,qhd->khd", grad_score, queries, preferred_element_type=jnp.float32)
    value_grad = jnp.einsum("hqk,qhd->khd", prob_half, grad_out, preferred_element_type=jnp.float32)

    both = jnp.concatenate(
        [
            key_grad.reshape(block_count, row_count, head_count * D_NOPE),
            value_grad.reshape(block_count, row_count, head_count * D_V),
        ],
        axis=2,
    )
    flat = scatter_sum(both, "blk").astype(jnp.bfloat16)
    key_flat = flat[:, : head_count * D_NOPE]
    value_flat = flat[:, head_count * D_NOPE :]

    def back_project(grad_flat, weight):
        return lax.dot_general(
            grad_flat, weight, (((1,), (1,)), ((), ())), preferred_element_type=jnp.float32
        )

    latent_part = back_project(key_flat, w_uk) + back_project(value_flat, w_uv)
    latent_sum = total_over(latent_part, "heads")
    grad_latent = (latent_sum * factor).astype(jnp.bfloat16)

    flats = gather_blocks(flat, "blk")
    comp_blocks = comp_all.reshape(block_count, row_count, col_width)
    weight_sum = jnp.zeros((col_width, flat.shape[1]), jnp.float32)
    for start in range(0, block_count, W_CHUNK):
        stop = min(start + W_CHUNK, block_count)
        product = jnp.einsum(
            "btl,btk->blk",
            comp_blocks[start:stop],
            flats[start:stop],
            preferred_element_type=jnp.float32,
        )
        rounded = product.astype(jnp.bfloat16).astype(jnp.float32)
        for index in range(stop - start):
            weight_sum = weight_sum + rounded[index]
    weight_key_grad = weight_sum[:, : head_count * D_NOPE]
    weight_value_grad = weight_sum[:, head_count * D_NOPE :]

    grad_q_nope = query_grad.reshape(row_count, head_count * D_NOPE).astype(jnp.bfloat16)
    grad_q_rope = rope_grad.reshape(row_count, head_count * D_ROPE).astype(jnp.bfloat16)
    return (grad_q_nope, grad_q_rope, grad_latent, weight_key_grad, weight_value_grad)


def solution(mesh):
    in_specs = (
        P("blk", "heads"),
        P("blk", "heads"),
        P("blk", "heads"),
        P("blk", None),
        P(None, "blk"),
        P("blk"),
        P("blk"),
        P(None, "heads"),
        P(None, "heads"),
    )
    out_specs = (
        P("blk", "heads"),
        P("blk", "heads"),
        P("blk", None),
        P(None, "heads"),
        P(None, "heads"),
    )
    return jax.shard_map(body, mesh=mesh, in_specs=in_specs, out_specs=out_specs, check_vma=False)
```

```python
import jax
import jax.numpy as jnp
from jax import lax
from jax.sharding import PartitionSpec as P

D_ROPE = 64
D_NOPE = 128
D_V = 128
POS_SPLIT = 64


lowest = -1e30


def digits_of(size):
    found = []
    stride = 1
    rest = size
    for prime in (2, 3):
        if rest % prime == 0:
            found.append((prime, stride))
            stride *= prime
            rest //= prime
    prime = 2
    while rest > 1:
        while rest % prime == 0:
            found.append((prime, stride))
            stride *= prime
            rest //= prime
        prime += 1
    return found


def gather_order(size):
    found = digits_of(size)
    odd = [d for d in found if d[0] != 2]
    even = sorted([d for d in found if d[0] == 2], key=lambda d: -d[1])
    return odd + even


def digit_value(axis, radix, stride):
    return (lax.axis_index(axis) // stride) % radix


def shift_digit(x, axis, radix, stride, by):
    size = lax.axis_size(axis)
    pairs = []
    for i in range(size):
        r = (i // stride) % radix
        pairs.append((i, i + (((r + by) % radix) - r) * stride))
    return lax.ppermute(x, axis, pairs)


def ordered_pieces(own, axis, radix, stride):
    r = digit_value(axis, radix, stride)
    received = {by: shift_digit(own, axis, radix, stride, by) for by in range(1, radix)}
    return canonical(own, received, r, radix)


def canonical(own, received, r, radix):
    pieces = []
    for k in range(radix):
        piece = own
        for by in range(1, radix):
            piece = jnp.where((r - k) % radix == by, received[by], piece)
        pieces.append(piece)
    return pieces


def gather_relative(block, axis):
    buf = block
    for radix, stride in gather_order(lax.axis_size(axis)):
        received = [shift_digit(buf, axis, radix, stride, by) for by in range(1, radix)]
        pieces = [buf] + [received[radix - k - 1] for k in range(1, radix)]
        buf = jnp.stack(pieces, axis=0)
    return buf


def scatter_relative(data, axis, lead, wire):
    level = 0
    for radix, stride in reversed(gather_order(lax.axis_size(axis))):
        head = (slice(None),) * lead
        total = data[head + (0,)]
        for by in range(1, radix):
            part = data[head + (by,)]
            if level > 0:
                part = part.astype(wire)
            total = total + shift_digit(part, axis, radix, stride, by).astype(jnp.float32)
        data = total
        level += 1
    return data


def total_over(x, axis):
    size = lax.axis_size(axis)
    for radix, stride in digits_of(size):
        if radix == 2:
            x = x + shift_digit(x, axis, radix, stride, 1)
        else:
            pieces = ordered_pieces(x, axis, radix, stride)
            x = pieces[0]
            for piece in pieces[1:]:
                x = x + piece
    return x


def body(q_nope, q_rope, d_out, latent, scale_exp, positions, spans, w_uk, w_uv):
    row_count = q_nope.shape[0]
    head_count = w_uk.shape[1] // D_NOPE
    col_width = latent.shape[1] - D_ROPE
    col_group = col_width // scale_exp.shape[0]
    block_count = lax.axis_size("blk")
    key_count = row_count * block_count
    soft_scale = (D_NOPE + D_ROPE) ** (-0.5)

    factor = jnp.exp2(jnp.repeat(jnp.transpose(scale_exp), col_group, axis=1).astype(jnp.float32))
    compressed = (latent[:, :col_width].astype(jnp.float32) * factor).astype(jnp.bfloat16)
    pos_hi = (positions // POS_SPLIT).astype(jnp.bfloat16)
    pos_lo = (positions % POS_SPLIT).astype(jnp.bfloat16)
    packed = jnp.concatenate(
        [compressed, latent[:, col_width:], pos_hi[:, None], pos_lo[:, None]], axis=1
    )
    everything = gather_relative(packed, "blk").reshape(key_count, packed.shape[1])
    comp_all = everything[:, :col_width]
    rope_all = everything[:, col_width : col_width + D_ROPE]
    key_pos = everything[:, col_width + D_ROPE].astype(jnp.int32) * POS_SPLIT + everything[
        :, col_width + D_ROPE + 1
    ].astype(jnp.int32)

    keys = jnp.dot(comp_all, w_uk, preferred_element_type=jnp.float32).astype(jnp.bfloat16)
    values = jnp.dot(comp_all, w_uv, preferred_element_type=jnp.float32).astype(jnp.bfloat16)
    keys = keys.reshape(key_count, head_count, D_NOPE)
    values = values.reshape(key_count, head_count, D_V)
    queries = q_nope.reshape(row_count, head_count, D_NOPE)
    query_rope = q_rope.reshape(row_count, head_count, D_ROPE)
    grad_out = d_out.reshape(row_count, head_count, D_V)

    scores = jnp.einsum("qhd,khd->hqk", queries, keys, preferred_element_type=jnp.float32)
    scores = scores + jnp.einsum(
        "qhr,kr->hqk", query_rope, rope_all, preferred_element_type=jnp.float32
    )
    scores = scores * soft_scale
    pairs = (key_pos[None, :] <= positions[:, None]) & (
        key_pos[None, :] >= positions[:, None] - spans[:, None]
    )
    masked = jnp.where(pairs[None], scores, lowest)
    row_max = jnp.max(masked, axis=2, keepdims=True)
    row_sum = jnp.sum(
        jnp.where(pairs[None], jnp.exp(masked - row_max), 0.0), axis=2, keepdims=True
    )
    log_norm = row_max + jnp.log(row_sum)
    prob_float = jnp.where(pairs[None], jnp.exp(scores - log_norm), 0.0)
    grad_prob = jnp.einsum("qhd,khd->hqk", grad_out, values, preferred_element_type=jnp.float32)
    delta_rows = jnp.sum(prob_float * grad_prob, axis=2, keepdims=True)
    grad_score = (prob_float * (grad_prob - delta_rows) * soft_scale).astype(jnp.bfloat16)
    prob_half = prob_float.astype(jnp.bfloat16)

    query_grad = jnp.einsum("hqk,khd->qhd", grad_score, keys, preferred_element_type=jnp.float32)
    rope_grad = jnp.einsum("hqk,kr->qhr", grad_score, rope_all, preferred_element_type=jnp.float32)
    stacked_left = jnp.stack([grad_score, prob_half], axis=0)
    stacked_right = jnp.stack(
        [jnp.transpose(queries, (1, 0, 2)), jnp.transpose(grad_out, (1, 0, 2))], axis=0
    )
    both = jnp.einsum(
        "ghqk,ghqd->ghkd", stacked_left, stacked_right, preferred_element_type=jnp.float32
    )
    radices = tuple(d[0] for d in reversed(gather_order(block_count)))
    both = both.reshape(both.shape[:2] + radices + (row_count, both.shape[3]))
    mine = scatter_relative(both, "blk", 2, jnp.bfloat16)
    mine = jnp.transpose(mine, (2, 0, 1, 3)).reshape(row_count, -1)
    flat = mine.astype(jnp.bfloat16)
    key_flat = flat[:, : head_count * D_NOPE]
    value_flat = flat[:, head_count * D_NOPE :]

    def back_project(grad_flat, weight):
        return lax.dot_general(
            grad_flat, weight, (((1,), (1,)), ((), ())), preferred_element_type=jnp.float32
        )

    latent_part = back_project(key_flat, w_uk) + back_project(value_flat, w_uv)
    latent_sum = total_over(latent_part, "heads")
    grad_latent = (latent_sum * factor).astype(jnp.bfloat16)

    flats = gather_relative(flat, "blk")
    order = gather_order(block_count)
    first_radix, first_stride = order[0]
    lead = radices[:-1]
    comp_rel = comp_all.reshape(radices + (row_count, col_width))
    slot_sums = []
    for slot in range(first_radix):
        left = comp_rel[..., slot, :, :].reshape((-1, row_count, col_width))
        right = flats[..., slot, :, :].reshape((-1, row_count, flat.shape[1]))
        product = jnp.einsum("btl,btk->blk", left, right, preferred_element_type=jnp.float32)
        partial = product.astype(jnp.bfloat16).astype(jnp.float32)
        partial = partial.reshape(lead + partial.shape[1:])
        for unused in lead:
            partial = partial[0] + partial[1]
        slot_sums.append(partial)
    first_digit = digit_value("blk", first_radix, first_stride)
    received = {by: slot_sums[first_radix - by] for by in range(1, first_radix)}
    ordered = canonical(slot_sums[0], received, first_digit, first_radix)
    weight_sum = ordered[0]
    for piece in ordered[1:]:
        weight_sum = weight_sum + piece
    weight_key_grad = weight_sum[:, : head_count * D_NOPE]
    weight_value_grad = weight_sum[:, head_count * D_NOPE :]

    grad_q_nope = query_grad.reshape(row_count, head_count * D_NOPE).astype(jnp.bfloat16)
    grad_q_rope = rope_grad.reshape(row_count, head_count * D_ROPE).astype(jnp.bfloat16)
    return (grad_q_nope, grad_q_rope, grad_latent, weight_key_grad, weight_value_grad)


def solution(mesh):
    in_specs = (
        P("blk", "heads"),
        P("blk", "heads"),
        P("blk", "heads"),
        P("blk", None),
        P(None, "blk"),
        P("blk"),
        P("blk"),
        P(None, "heads"),
        P(None, "heads"),
    )
    out_specs = (
        P("blk", "heads"),
        P("blk", "heads"),
        P("blk", None),
        P(None, "heads"),
        P(None, "heads"),
    )
    return jax.shard_map(body, mesh=mesh, in_specs=in_specs, out_specs=out_specs, check_vma=False)
```

```python
import jax
import jax.numpy as jnp
from jax import lax
from jax.sharding import PartitionSpec as P

D_ROPE = 64
D_NOPE = 128
D_V = 128
POS_SPLIT = 64


lowest = -1e30


def digits_of(size):
    found = []
    stride = 1
    rest = size
    for prime in (2, 3):
        if rest % prime == 0:
            found.append((prime, stride))
            stride *= prime
            rest //= prime
    while rest % 4 == 0:
        found.append((4, stride))
        stride *= 4
        rest //= 4
    prime = 2
    while rest > 1:
        while rest % prime == 0:
            found.append((prime, stride))
            stride *= prime
            rest //= prime
        prime += 1
    return found


def gather_order(size):
    return sorted(digits_of(size), key=lambda d: (d[0] != 3, -d[1]))


def digit_value(axis, radix, stride):
    return (lax.axis_index(axis) // stride) % radix


def shift_digit(x, axis, radix, stride, by):
    size = lax.axis_size(axis)
    pairs = []
    for i in range(size):
        r = (i // stride) % radix
        pairs.append((i, i + (((r + by) % radix) - r) * stride))
    return lax.ppermute(x, axis, pairs)


def ordered_pieces(own, axis, radix, stride):
    r = digit_value(axis, radix, stride)
    received = {by: shift_digit(own, axis, radix, stride, by) for by in range(1, radix)}
    return canonical(own, received, r, radix)


def canonical(own, received, r, radix):
    pieces = []
    for k in range(radix):
        piece = own
        for by in range(1, radix):
            piece = jnp.where((r - k) % radix == by, received[by], piece)
        pieces.append(piece)
    return pieces


def gather_relative(block, axis):
    buf = block
    for radix, stride in gather_order(lax.axis_size(axis)):
        received = [shift_digit(buf, axis, radix, stride, by) for by in range(1, radix)]
        pieces = [buf] + [received[radix - k - 1] for k in range(1, radix)]
        buf = jnp.stack(pieces, axis=0)
    return buf


def scatter_relative(data, axis, lead, wire):
    level = 0
    for radix, stride in reversed(gather_order(lax.axis_size(axis))):
        head = (slice(None),) * lead
        total = data[head + (0,)]
        for by in range(1, radix):
            part = data[head + (by,)]
            if level > 0:
                part = part.astype(wire)
            total = total + shift_digit(part, axis, radix, stride, by).astype(jnp.float32)
        data = total
        level += 1
    return data


def ordered_sum(slots, axis, radix, stride):
    r = digit_value(axis, radix, stride)
    received = {by: slots[radix - by] for by in range(1, radix)}
    ordered = canonical(slots[0], received, r, radix)
    total = ordered[0]
    for piece in ordered[1:]:
        total = total + piece
    return total


def total_over(x, axis):
    size = lax.axis_size(axis)
    for radix, stride in digits_of(size):
        if radix == 2:
            x = x + shift_digit(x, axis, radix, stride, 1)
        else:
            pieces = ordered_pieces(x, axis, radix, stride)
            x = pieces[0]
            for piece in pieces[1:]:
                x = x + piece
    return x


def body(q_nope, q_rope, d_out, latent, scale_exp, positions, spans, w_uk, w_uv):
    row_count = q_nope.shape[0]
    head_count = w_uk.shape[1] // D_NOPE
    col_width = latent.shape[1] - D_ROPE
    col_group = col_width // scale_exp.shape[0]
    block_count = lax.axis_size("blk")
    key_count = row_count * block_count
    soft_scale = (D_NOPE + D_ROPE) ** (-0.5)

    factor = jnp.exp2(jnp.repeat(jnp.transpose(scale_exp), col_group, axis=1).astype(jnp.float32))
    compressed = (latent[:, :col_width].astype(jnp.float32) * factor).astype(jnp.bfloat16)
    pos_hi = (positions // POS_SPLIT).astype(jnp.bfloat16)
    pos_lo = (positions % POS_SPLIT).astype(jnp.bfloat16)
    packed = jnp.concatenate(
        [compressed, latent[:, col_width:], pos_hi[:, None], pos_lo[:, None]], axis=1
    )
    everything = gather_relative(packed, "blk").reshape(key_count, packed.shape[1])
    comp_all = everything[:, :col_width]
    rope_all = everything[:, col_width : col_width + D_ROPE]
    key_pos = everything[:, col_width + D_ROPE].astype(jnp.int32) * POS_SPLIT + everything[
        :, col_width + D_ROPE + 1
    ].astype(jnp.int32)

    keys = jnp.dot(comp_all, w_uk, preferred_element_type=jnp.float32).astype(jnp.bfloat16)
    values = jnp.dot(comp_all, w_uv, preferred_element_type=jnp.float32).astype(jnp.bfloat16)
    keys = keys.reshape(key_count, head_count, D_NOPE)
    values = values.reshape(key_count, head_count, D_V)
    queries = q_nope.reshape(row_count, head_count, D_NOPE)
    query_rope = q_rope.reshape(row_count, head_count, D_ROPE)
    grad_out = d_out.reshape(row_count, head_count, D_V)

    scores = jnp.einsum("qhd,khd->hqk", queries, keys, preferred_element_type=jnp.float32)
    scores = scores + jnp.einsum(
        "qhr,kr->hqk", query_rope, rope_all, preferred_element_type=jnp.float32
    )
    scores = scores * soft_scale
    pairs = (key_pos[None, :] <= positions[:, None]) & (
        key_pos[None, :] >= positions[:, None] - spans[:, None]
    )
    masked = jnp.where(pairs[None], scores, lowest)
    row_max = jnp.max(masked, axis=2, keepdims=True)
    row_sum = jnp.sum(
        jnp.where(pairs[None], jnp.exp(masked - row_max), 0.0), axis=2, keepdims=True
    )
    log_norm = row_max + jnp.log(row_sum)
    prob_float = jnp.where(pairs[None], jnp.exp(scores - log_norm), 0.0)
    grad_prob = jnp.einsum("qhd,khd->hqk", grad_out, values, preferred_element_type=jnp.float32)
    delta_rows = jnp.sum(prob_float * grad_prob, axis=2, keepdims=True)
    grad_score = (prob_float * (grad_prob - delta_rows) * soft_scale).astype(jnp.bfloat16)
    prob_half = prob_float.astype(jnp.bfloat16)

    query_grad = jnp.einsum("hqk,khd->qhd", grad_score, keys, preferred_element_type=jnp.float32)
    rope_grad = jnp.einsum("hqk,kr->qhr", grad_score, rope_all, preferred_element_type=jnp.float32)
    stacked_left = jnp.stack([grad_score, prob_half], axis=0)
    stacked_right = jnp.stack(
        [jnp.transpose(queries, (1, 0, 2)), jnp.transpose(grad_out, (1, 0, 2))], axis=0
    )
    both = jnp.einsum(
        "ghqk,ghqd->ghkd", stacked_left, stacked_right, preferred_element_type=jnp.float32
    )
    radices = tuple(d[0] for d in reversed(gather_order(block_count)))
    both = both.reshape(both.shape[:2] + radices + (row_count, both.shape[3]))
    mine = scatter_relative(both, "blk", 2, jnp.bfloat16)
    mine = jnp.transpose(mine, (2, 0, 1, 3)).reshape(row_count, -1)
    flat = mine.astype(jnp.bfloat16)
    key_flat = flat[:, : head_count * D_NOPE]
    value_flat = flat[:, head_count * D_NOPE :]

    def back_project(grad_flat, weight):
        return lax.dot_general(
            grad_flat, weight, (((1,), (1,)), ((), ())), preferred_element_type=jnp.float32
        )

    latent_part = back_project(key_flat, w_uk) + back_project(value_flat, w_uv)
    latent_sum = total_over(latent_part, "heads")
    grad_latent = (latent_sum * factor).astype(jnp.bfloat16)

    flats = gather_relative(flat, "blk")
    order = gather_order(block_count)
    first_radix, first_stride = order[0]
    lead = radices[:-1]
    lead_digits = list(reversed(order))[:-1]
    comp_rel = comp_all.reshape(radices + (row_count, col_width))
    slot_sums = []
    for slot in range(first_radix):
        left = comp_rel[..., slot, :, :].reshape((-1, row_count, col_width))
        right = flats[..., slot, :, :].reshape((-1, row_count, flat.shape[1]))
        product = jnp.einsum("btl,btk->blk", left, right, preferred_element_type=jnp.float32)
        partial = product.astype(jnp.bfloat16).astype(jnp.float32)
        partial = partial.reshape(lead + partial.shape[1:])
        for radix, stride in lead_digits:
            partial = ordered_sum([partial[k] for k in range(radix)], "blk", radix, stride)
        slot_sums.append(partial)
    weight_sum = ordered_sum(slot_sums, "blk", first_radix, first_stride)
    weight_key_grad = weight_sum[:, : head_count * D_NOPE]
    weight_value_grad = weight_sum[:, head_count * D_NOPE :]

    grad_q_nope = query_grad.reshape(row_count, head_count * D_NOPE).astype(jnp.bfloat16)
    grad_q_rope = rope_grad.reshape(row_count, head_count * D_ROPE).astype(jnp.bfloat16)
    return (grad_q_nope, grad_q_rope, grad_latent, weight_key_grad, weight_value_grad)


def solution(mesh):
    in_specs = (
        P("blk", "heads"),
        P("blk", "heads"),
        P("blk", "heads"),
        P("blk", None),
        P(None, "blk"),
        P("blk"),
        P("blk"),
        P(None, "heads"),
        P(None, "heads"),
    )
    out_specs = (
        P("blk", "heads"),
        P("blk", "heads"),
        P("blk", None),
        P(None, "heads"),
        P(None, "heads"),
    )
    return jax.shard_map(body, mesh=mesh, in_specs=in_specs, out_specs=out_specs, check_vma=False)
```

```python
import jax
import jax.numpy as jnp
from jax import lax
from jax.sharding import PartitionSpec as P

D_ROPE = 64
D_NOPE = 128
D_V = 128
POS_SPLIT = 64


lowest = -1e30


def digits_of(size):
    found = []
    stride = 1
    rest = size
    for prime in (2, 3):
        if rest % prime == 0:
            found.append((prime, stride))
            stride *= prime
            rest //= prime
    while rest % 4 == 0:
        found.append((4, stride))
        stride *= 4
        rest //= 4
    prime = 2
    while rest > 1:
        while rest % prime == 0:
            found.append((prime, stride))
            stride *= prime
            rest //= prime
        prime += 1
    return found


def gather_order(size):
    return sorted(digits_of(size), key=lambda d: (d[0] != 3, -d[1]))


def digit_value(axis, radix, stride):
    return (lax.axis_index(axis) // stride) % radix


def shift_digit(x, axis, radix, stride, by):
    size = lax.axis_size(axis)
    pairs = []
    for i in range(size):
        r = (i // stride) % radix
        pairs.append((i, i + (((r + by) % radix) - r) * stride))
    return lax.ppermute(x, axis, pairs)


def ordered_pieces(own, axis, radix, stride):
    r = digit_value(axis, radix, stride)
    received = {by: shift_digit(own, axis, radix, stride, by) for by in range(1, radix)}
    return canonical(own, received, r, radix)


def canonical(own, received, r, radix):
    pieces = []
    for k in range(radix):
        piece = own
        for by in range(1, radix):
            piece = jnp.where((r - k) % radix == by, received[by], piece)
        pieces.append(piece)
    return pieces


def gather_step(buf, axis, radix, stride):
    received = [shift_digit(buf, axis, radix, stride, by) for by in range(1, radix)]
    pieces = [buf] + [received[radix - k - 1] for k in range(1, radix)]
    return jnp.stack(pieces, axis=0)


def gather_relative(block, axis):
    buf = block
    for radix, stride in gather_order(lax.axis_size(axis)):
        buf = gather_step(buf, axis, radix, stride)
    return buf


def scatter_relative(data, axis, lead, wire):
    level = 0
    for radix, stride in reversed(gather_order(lax.axis_size(axis))):
        head = (slice(None),) * lead
        total = data[head + (0,)]
        for by in range(1, radix):
            part = data[head + (by,)]
            if level > 0:
                part = part.astype(wire)
            total = total + shift_digit(part, axis, radix, stride, by).astype(jnp.float32)
        data = total
        level += 1
    return data


def ordered_sum(slots, axis, radix, stride):
    r = digit_value(axis, radix, stride)
    received = {by: slots[radix - by] for by in range(1, radix)}
    ordered = canonical(slots[0], received, r, radix)
    total = ordered[0]
    for piece in ordered[1:]:
        total = total + piece
    return total


def reduce_step(x, axis, radix, stride):
    if radix == 2:
        return x + shift_digit(x, axis, radix, stride, 1)
    pieces = ordered_pieces(x, axis, radix, stride)
    total = pieces[0]
    for piece in pieces[1:]:
        total = total + piece
    return total


def body(q_nope, q_rope, d_out, latent, scale_exp, positions, spans, w_uk, w_uv):
    row_count = q_nope.shape[0]
    head_count = w_uk.shape[1] // D_NOPE
    col_width = latent.shape[1] - D_ROPE
    col_group = col_width // scale_exp.shape[0]
    block_count = lax.axis_size("blk")
    key_count = row_count * block_count
    soft_scale = (D_NOPE + D_ROPE) ** (-0.5)

    factor = jnp.exp2(jnp.repeat(jnp.transpose(scale_exp), col_group, axis=1).astype(jnp.float32))
    compressed = (latent[:, :col_width].astype(jnp.float32) * factor).astype(jnp.bfloat16)
    pos_hi = (positions // POS_SPLIT).astype(jnp.bfloat16)
    pos_lo = (positions % POS_SPLIT).astype(jnp.bfloat16)
    packed = jnp.concatenate(
        [compressed, latent[:, col_width:], pos_hi[:, None], pos_lo[:, None]], axis=1
    )
    everything = gather_relative(packed, "blk").reshape(key_count, packed.shape[1])
    comp_all = everything[:, :col_width]
    rope_all = everything[:, col_width : col_width + D_ROPE]
    key_pos = everything[:, col_width + D_ROPE].astype(jnp.int32) * POS_SPLIT + everything[
        :, col_width + D_ROPE + 1
    ].astype(jnp.int32)

    keys = jnp.dot(comp_all, w_uk, preferred_element_type=jnp.float32).astype(jnp.bfloat16)
    values = jnp.dot(comp_all, w_uv, preferred_element_type=jnp.float32).astype(jnp.bfloat16)
    keys = keys.reshape(key_count, head_count, D_NOPE)
    values = values.reshape(key_count, head_count, D_V)
    queries = q_nope.reshape(row_count, head_count, D_NOPE)
    query_rope = q_rope.reshape(row_count, head_count, D_ROPE)
    grad_out = d_out.reshape(row_count, head_count, D_V)

    scores = jnp.einsum("qhd,khd->hqk", queries, keys, preferred_element_type=jnp.float32)
    scores = scores + jnp.einsum(
        "qhr,kr->hqk", query_rope, rope_all, preferred_element_type=jnp.float32
    )
    scores = scores * soft_scale
    pairs = (key_pos[None, :] <= positions[:, None]) & (
        key_pos[None, :] >= positions[:, None] - spans[:, None]
    )
    masked = jnp.where(pairs[None], scores, lowest)
    row_max = jnp.max(masked, axis=2, keepdims=True)
    row_sum = jnp.sum(
        jnp.where(pairs[None], jnp.exp(masked - row_max), 0.0), axis=2, keepdims=True
    )
    log_norm = row_max + jnp.log(row_sum)
    prob_float = jnp.where(pairs[None], jnp.exp(scores - log_norm), 0.0)
    grad_prob = jnp.einsum("qhd,khd->hqk", grad_out, values, preferred_element_type=jnp.float32)
    delta_rows = jnp.sum(prob_float * grad_prob, axis=2, keepdims=True)
    grad_score = (prob_float * (grad_prob - delta_rows) * soft_scale).astype(jnp.bfloat16)
    prob_half = prob_float.astype(jnp.bfloat16)

    query_grad = jnp.einsum("hqk,khd->qhd", grad_score, keys, preferred_element_type=jnp.float32)
    rope_grad = jnp.einsum("hqk,kr->qhr", grad_score, rope_all, preferred_element_type=jnp.float32)
    stacked_left = jnp.stack([grad_score, prob_half], axis=0)
    stacked_right = jnp.stack(
        [jnp.transpose(queries, (1, 0, 2)), jnp.transpose(grad_out, (1, 0, 2))], axis=0
    )
    both = jnp.einsum(
        "ghqk,ghqd->ghkd", stacked_left, stacked_right, preferred_element_type=jnp.float32
    )
    radices = tuple(d[0] for d in reversed(gather_order(block_count)))
    both = both.reshape(both.shape[:2] + radices + (row_count, both.shape[3]))
    mine = scatter_relative(both, "blk", 2, jnp.bfloat16)
    mine = jnp.transpose(mine, (2, 0, 1, 3)).reshape(row_count, -1)
    flat = mine.astype(jnp.bfloat16)
    key_flat = flat[:, : head_count * D_NOPE]
    value_flat = flat[:, head_count * D_NOPE :]

    def back_project(grad_flat, weight):
        return lax.dot_general(
            grad_flat, weight, (((1,), (1,)), ((), ())), preferred_element_type=jnp.float32
        )

    latent_part = back_project(key_flat, w_uk) + back_project(value_flat, w_uv)
    sum_levels = digits_of(lax.axis_size("heads"))
    gather_levels = gather_order(block_count)
    latent_sum = latent_part
    flats = flat
    for level in range(max(len(sum_levels), len(gather_levels))):
        if level < len(gather_levels):
            flats = gather_step(flats, "blk", *gather_levels[level])
        if level < len(sum_levels):
            latent_sum = reduce_step(latent_sum, "heads", *sum_levels[level])
        flats, latent_sum = lax.optimization_barrier((flats, latent_sum))
    grad_latent = (latent_sum * factor).astype(jnp.bfloat16)

    order = gather_order(block_count)
    first_radix, first_stride = order[0]
    lead = radices[:-1]
    lead_digits = list(reversed(order))[:-1]
    comp_rel = comp_all.reshape(radices + (row_count, col_width))
    slot_sums = []
    for slot in range(first_radix):
        left = comp_rel[..., slot, :, :].reshape((-1, row_count, col_width))
        right = flats[..., slot, :, :].reshape((-1, row_count, flat.shape[1]))
        product = jnp.einsum("btl,btk->blk", left, right, preferred_element_type=jnp.float32)
        partial = product.astype(jnp.bfloat16).astype(jnp.float32)
        partial = partial.reshape(lead + partial.shape[1:])
        for radix, stride in lead_digits:
            partial = ordered_sum([partial[k] for k in range(radix)], "blk", radix, stride)
        slot_sums.append(partial)
    weight_sum = ordered_sum(slot_sums, "blk", first_radix, first_stride)
    weight_key_grad = weight_sum[:, : head_count * D_NOPE]
    weight_value_grad = weight_sum[:, head_count * D_NOPE :]

    grad_q_nope = query_grad.reshape(row_count, head_count * D_NOPE).astype(jnp.bfloat16)
    grad_q_rope = rope_grad.reshape(row_count, head_count * D_ROPE).astype(jnp.bfloat16)
    return (grad_q_nope, grad_q_rope, grad_latent, weight_key_grad, weight_value_grad)


def solution(mesh):
    in_specs = (
        P("blk", "heads"),
        P("blk", "heads"),
        P("blk", "heads"),
        P("blk", None),
        P(None, "blk"),
        P("blk"),
        P("blk"),
        P(None, "heads"),
        P(None, "heads"),
    )
    out_specs = (
        P("blk", "heads"),
        P("blk", "heads"),
        P("blk", None),
        P(None, "heads"),
        P(None, "heads"),
    )
    return jax.shard_map(body, mesh=mesh, in_specs=in_specs, out_specs=out_specs, check_vma=False)
```

```python
import jax
import jax.numpy as jnp
from jax import lax
from jax.sharding import PartitionSpec as P

D_ROPE = 64
D_NOPE = 128
D_V = 128
POS_SPLIT = 64


lowest = -1e30


def digits_of(size):
    found = []
    stride = 1
    rest = size
    for prime in (2, 3):
        if rest % prime == 0:
            found.append((prime, stride))
            stride *= prime
            rest //= prime
    while rest % 4 == 0:
        found.append((4, stride))
        stride *= 4
        rest //= 4
    prime = 2
    while rest > 1:
        while rest % prime == 0:
            found.append((prime, stride))
            stride *= prime
            rest //= prime
        prime += 1
    return found


def gather_order(size):
    return sorted(digits_of(size), key=lambda d: (d[0] != 3, -d[1]))


def digit_value(axis, radix, stride):
    return (lax.axis_index(axis) // stride) % radix


def shift_digit(x, axis, radix, stride, by):
    size = lax.axis_size(axis)
    pairs = []
    for i in range(size):
        r = (i // stride) % radix
        pairs.append((i, i + (((r + by) % radix) - r) * stride))
    return lax.ppermute(x, axis, pairs)


def ordered_pieces(own, axis, radix, stride):
    r = digit_value(axis, radix, stride)
    received = {by: shift_digit(own, axis, radix, stride, by) for by in range(1, radix)}
    return canonical(own, received, r, radix)


def canonical(own, received, r, radix):
    pieces = []
    for k in range(radix):
        piece = own
        for by in range(1, radix):
            piece = jnp.where((r - k) % radix == by, received[by], piece)
        pieces.append(piece)
    return pieces


def gather_step(buf, axis, radix, stride):
    received = [shift_digit(buf, axis, radix, stride, by) for by in range(1, radix)]
    pieces = [buf] + [received[radix - k - 1] for k in range(1, radix)]
    return jnp.stack(pieces, axis=0)


def gather_relative(block, axis):
    buf = block
    for radix, stride in gather_order(lax.axis_size(axis)):
        buf = gather_step(buf, axis, radix, stride)
    return buf


def scatter_relative(data, axis, lead, wire):
    level = 0
    for radix, stride in reversed(gather_order(lax.axis_size(axis))):
        head = (slice(None),) * lead
        total = data[head + (0,)]
        for by in range(1, radix):
            part = data[head + (by,)]
            if level > 0:
                part = part.astype(wire)
            total = total + shift_digit(part, axis, radix, stride, by).astype(jnp.float32)
        data = total
        level += 1
    return data


def ordered_sum(slots, axis, radix, stride):
    r = digit_value(axis, radix, stride)
    received = {by: slots[radix - by] for by in range(1, radix)}
    ordered = canonical(slots[0], received, r, radix)
    total = ordered[0]
    for piece in ordered[1:]:
        total = total + piece
    return total


def reduce_step(x, axis, radix, stride, wire):
    own = x.astype(wire)
    if radix == 2:
        return own.astype(jnp.float32) + shift_digit(own, axis, radix, stride, 1).astype(jnp.float32)
    pieces = ordered_pieces(own, axis, radix, stride)
    total = pieces[0].astype(jnp.float32)
    for piece in pieces[1:]:
        total = total + piece.astype(jnp.float32)
    return total


def body(q_nope, q_rope, d_out, latent, scale_exp, positions, spans, w_uk, w_uv):
    row_count = q_nope.shape[0]
    head_count = w_uk.shape[1] // D_NOPE
    col_width = latent.shape[1] - D_ROPE
    col_group = col_width // scale_exp.shape[0]
    block_count = lax.axis_size("blk")
    key_count = row_count * block_count
    soft_scale = (D_NOPE + D_ROPE) ** (-0.5)

    factor = jnp.exp2(jnp.repeat(jnp.transpose(scale_exp), col_group, axis=1).astype(jnp.float32))
    compressed = (latent[:, :col_width].astype(jnp.float32) * factor).astype(jnp.bfloat16)
    pos_hi = (positions // POS_SPLIT).astype(jnp.bfloat16)
    pos_lo = (positions % POS_SPLIT).astype(jnp.bfloat16)
    packed = jnp.concatenate(
        [compressed, latent[:, col_width:], pos_hi[:, None], pos_lo[:, None]], axis=1
    )
    everything = gather_relative(packed, "blk").reshape(key_count, packed.shape[1])
    comp_all = everything[:, :col_width]
    rope_all = everything[:, col_width : col_width + D_ROPE]
    key_pos = everything[:, col_width + D_ROPE].astype(jnp.int32) * POS_SPLIT + everything[
        :, col_width + D_ROPE + 1
    ].astype(jnp.int32)

    keys = jnp.dot(comp_all, w_uk, preferred_element_type=jnp.float32).astype(jnp.bfloat16)
    values = jnp.dot(comp_all, w_uv, preferred_element_type=jnp.float32).astype(jnp.bfloat16)
    keys = keys.reshape(key_count, head_count, D_NOPE)
    values = values.reshape(key_count, head_count, D_V)
    queries = q_nope.reshape(row_count, head_count, D_NOPE)
    query_rope = q_rope.reshape(row_count, head_count, D_ROPE)
    grad_out = d_out.reshape(row_count, head_count, D_V)

    scores = jnp.einsum("qhd,khd->hqk", queries, keys, preferred_element_type=jnp.float32)
    scores = scores + jnp.einsum(
        "qhr,kr->hqk", query_rope, rope_all, preferred_element_type=jnp.float32
    )
    scores = scores * soft_scale
    pairs = (key_pos[None, :] <= positions[:, None]) & (
        key_pos[None, :] >= positions[:, None] - spans[:, None]
    )
    masked = jnp.where(pairs[None], scores, lowest)
    row_max = jnp.max(masked, axis=2, keepdims=True)
    row_sum = jnp.sum(
        jnp.where(pairs[None], jnp.exp(masked - row_max), 0.0), axis=2, keepdims=True
    )
    log_norm = row_max + jnp.log(row_sum)
    prob_float = jnp.where(pairs[None], jnp.exp(scores - log_norm), 0.0)
    grad_prob = jnp.einsum("qhd,khd->hqk", grad_out, values, preferred_element_type=jnp.float32)
    delta_rows = jnp.sum(prob_float * grad_prob, axis=2, keepdims=True)
    grad_score = (prob_float * (grad_prob - delta_rows) * soft_scale).astype(jnp.bfloat16)
    prob_half = prob_float.astype(jnp.bfloat16)

    query_grad = jnp.einsum("hqk,khd->qhd", grad_score, keys, preferred_element_type=jnp.float32)
    rope_grad = jnp.einsum("hqk,kr->qhr", grad_score, rope_all, preferred_element_type=jnp.float32)
    stacked_left = jnp.stack([grad_score, prob_half], axis=0)
    stacked_right = jnp.stack(
        [jnp.transpose(queries, (1, 0, 2)), jnp.transpose(grad_out, (1, 0, 2))], axis=0
    )
    both = jnp.einsum(
        "ghqk,ghqd->ghkd", stacked_left, stacked_right, preferred_element_type=jnp.float32
    )
    radices = tuple(d[0] for d in reversed(gather_order(block_count)))
    both = both.reshape(both.shape[:2] + radices + (row_count, both.shape[3]))
    mine = scatter_relative(both, "blk", 2, jnp.bfloat16)
    mine = jnp.transpose(mine, (2, 0, 1, 3)).reshape(row_count, -1)
    flat = mine.astype(jnp.bfloat16)
    key_flat = flat[:, : head_count * D_NOPE]
    value_flat = flat[:, head_count * D_NOPE :]

    def back_project(grad_flat, weight):
        return lax.dot_general(
            grad_flat, weight, (((1,), (1,)), ((), ())), preferred_element_type=jnp.float32
        )

    latent_part = back_project(key_flat, w_uk) + back_project(value_flat, w_uv)
    sum_levels = digits_of(lax.axis_size("heads"))
    gather_levels = gather_order(block_count)
    latent_sum = latent_part
    flats = flat
    for level in range(max(len(sum_levels), len(gather_levels))):
        if level < len(gather_levels):
            flats = gather_step(flats, "blk", *gather_levels[level])
        if level < len(sum_levels):
            latent_sum = reduce_step(latent_sum, "heads", *sum_levels[level], jnp.bfloat16)
        flats, latent_sum = lax.optimization_barrier((flats, latent_sum))
    grad_latent = (latent_sum * factor).astype(jnp.bfloat16)

    order = gather_order(block_count)
    first_radix, first_stride = order[0]
    lead = radices[:-1]
    lead_digits = list(reversed(order))[:-1]
    comp_rel = comp_all.reshape(radices + (row_count, col_width))
    slot_sums = []
    for slot in range(first_radix):
        left = comp_rel[..., slot, :, :].reshape((-1, row_count, col_width))
        right = flats[..., slot, :, :].reshape((-1, row_count, flat.shape[1]))
        product = jnp.einsum("btl,btk->blk", left, right, preferred_element_type=jnp.float32)
        partial = product.astype(jnp.bfloat16).astype(jnp.float32)
        partial = partial.reshape(lead + partial.shape[1:])
        for radix, stride in lead_digits:
            partial = ordered_sum([partial[k] for k in range(radix)], "blk", radix, stride)
        slot_sums.append(partial)
    weight_sum = ordered_sum(slot_sums, "blk", first_radix, first_stride)
    weight_key_grad = weight_sum[:, : head_count * D_NOPE]
    weight_value_grad = weight_sum[:, head_count * D_NOPE :]

    grad_q_nope = query_grad.reshape(row_count, head_count * D_NOPE).astype(jnp.bfloat16)
    grad_q_rope = rope_grad.reshape(row_count, head_count * D_ROPE).astype(jnp.bfloat16)
    return (grad_q_nope, grad_q_rope, grad_latent, weight_key_grad, weight_value_grad)


def solution(mesh):
    in_specs = (
        P("blk", "heads"),
        P("blk", "heads"),
        P("blk", "heads"),
        P("blk", None),
        P(None, "blk"),
        P("blk"),
        P("blk"),
        P(None, "heads"),
        P(None, "heads"),
    )
    out_specs = (
        P("blk", "heads"),
        P("blk", "heads"),
        P("blk", None),
        P(None, "heads"),
        P(None, "heads"),
    )
    return jax.shard_map(body, mesh=mesh, in_specs=in_specs, out_specs=out_specs, check_vma=False)
```

```python
import jax
import jax.numpy as jnp
from jax import lax
from jax.sharding import PartitionSpec as P

D_ROPE = 64
D_NOPE = 128
D_V = 128
POS_SPLIT = 64


lowest = -1e30


def digits_of(size):
    found = []
    stride = 1
    rest = size
    for prime in (2, 3):
        if rest % prime == 0:
            found.append((prime, stride))
            stride *= prime
            rest //= prime
    while rest % 4 == 0:
        found.append((4, stride))
        stride *= 4
        rest //= 4
    prime = 2
    while rest > 1:
        while rest % prime == 0:
            found.append((prime, stride))
            stride *= prime
            rest //= prime
        prime += 1
    return found


def gather_order(size):
    return sorted(digits_of(size), key=lambda d: (d[0] != 3, -d[1]))


def digit_value(axis, radix, stride):
    return (lax.axis_index(axis) // stride) % radix


def shift_digit(x, axis, radix, stride, by):
    size = lax.axis_size(axis)
    pairs = []
    for i in range(size):
        r = (i // stride) % radix
        pairs.append((i, i + (((r + by) % radix) - r) * stride))
    return lax.ppermute(x, axis, pairs)


def ordered_pieces(own, axis, radix, stride):
    r = digit_value(axis, radix, stride)
    received = {by: shift_digit(own, axis, radix, stride, by) for by in range(1, radix)}
    return canonical(own, received, r, radix)


def canonical(own, received, r, radix):
    pieces = []
    for k in range(radix):
        piece = own
        for by in range(1, radix):
            piece = jnp.where((r - k) % radix == by, received[by], piece)
        pieces.append(piece)
    return pieces


def gather_step(buf, axis, radix, stride):
    received = [shift_digit(buf, axis, radix, stride, by) for by in range(1, radix)]
    pieces = [buf] + [received[radix - k - 1] for k in range(1, radix)]
    return jnp.stack(pieces, axis=0)


def gather_relative(block, axis):
    buf = block
    for radix, stride in gather_order(lax.axis_size(axis)):
        buf = gather_step(buf, axis, radix, stride)
    return buf


def scatter_relative(data, axis, lead, wire):
    level = 0
    for radix, stride in reversed(gather_order(lax.axis_size(axis))):
        head = (slice(None),) * lead
        total = data[head + (0,)]
        for by in range(1, radix):
            part = data[head + (by,)]
            if level > 0:
                part = part.astype(wire)
            total = total + shift_digit(part, axis, radix, stride, by).astype(jnp.float32)
        data = total
        level += 1
    return data


def ordered_sum(slots, axis, radix, stride):
    r = digit_value(axis, radix, stride)
    received = {by: slots[radix - by] for by in range(1, radix)}
    ordered = canonical(slots[0], received, r, radix)
    total = ordered[0]
    for piece in ordered[1:]:
        total = total + piece
    return total


def reduce_step(x, axis, radix, stride, wire):
    own = x.astype(wire)
    if radix == 2:
        return own.astype(jnp.float32) + shift_digit(own, axis, radix, stride, 1).astype(jnp.float32)
    pieces = ordered_pieces(own, axis, radix, stride)
    total = pieces[0].astype(jnp.float32)
    for piece in pieces[1:]:
        total = total + piece.astype(jnp.float32)
    return total


def body(q_nope, q_rope, d_out, latent, scale_exp, positions, spans, w_uk, w_uv):
    row_count = q_nope.shape[0]
    head_count = w_uk.shape[1] // D_NOPE
    col_width = latent.shape[1] - D_ROPE
    col_group = col_width // scale_exp.shape[0]
    block_count = lax.axis_size("blk")
    key_count = row_count * block_count
    soft_scale = (D_NOPE + D_ROPE) ** (-0.5)

    factor = jnp.exp2(jnp.repeat(jnp.transpose(scale_exp), col_group, axis=1).astype(jnp.float32))
    compressed = (latent[:, :col_width].astype(jnp.float32) * factor).astype(jnp.bfloat16)
    pos_hi = (positions // POS_SPLIT).astype(jnp.bfloat16)
    pos_lo = (positions % POS_SPLIT).astype(jnp.bfloat16)
    packed = jnp.concatenate(
        [compressed, latent[:, col_width:], pos_hi[:, None], pos_lo[:, None]], axis=1
    )
    everything = gather_relative(packed, "blk").reshape(key_count, packed.shape[1])
    comp_all = everything[:, :col_width]
    rope_all = everything[:, col_width : col_width + D_ROPE]
    key_pos = everything[:, col_width + D_ROPE].astype(jnp.int32) * POS_SPLIT + everything[
        :, col_width + D_ROPE + 1
    ].astype(jnp.int32)

    keys = jnp.dot(comp_all, w_uk, preferred_element_type=jnp.float32).astype(jnp.bfloat16)
    values = jnp.dot(comp_all, w_uv, preferred_element_type=jnp.float32).astype(jnp.bfloat16)
    keys = keys.reshape(key_count, head_count, D_NOPE)
    values = values.reshape(key_count, head_count, D_V)
    queries = q_nope.reshape(row_count, head_count, D_NOPE)
    query_rope = q_rope.reshape(row_count, head_count, D_ROPE)
    grad_out = d_out.reshape(row_count, head_count, D_V)

    scores = jnp.einsum("qhd,khd->hqk", queries, keys, preferred_element_type=jnp.float32)
    scores = scores + jnp.einsum(
        "qhr,kr->hqk", query_rope, rope_all, preferred_element_type=jnp.float32
    )
    scores = scores * soft_scale
    pairs = (key_pos[None, :] <= positions[:, None]) & (
        key_pos[None, :] >= positions[:, None] - spans[:, None]
    )
    masked = jnp.where(pairs[None], scores, lowest)
    row_max = jnp.max(masked, axis=2, keepdims=True)
    row_sum = jnp.sum(
        jnp.where(pairs[None], jnp.exp(masked - row_max), 0.0), axis=2, keepdims=True
    )
    log_norm = row_max + jnp.log(row_sum)
    prob_float = jnp.where(pairs[None], jnp.exp(scores - log_norm), 0.0)
    grad_prob = jnp.einsum("qhd,khd->hqk", grad_out, values, preferred_element_type=jnp.float32)
    delta_rows = jnp.sum(prob_float * grad_prob, axis=2, keepdims=True)
    grad_score = (prob_float * (grad_prob - delta_rows) * soft_scale).astype(jnp.bfloat16)
    prob_half = prob_float.astype(jnp.bfloat16)

    query_grad = jnp.einsum("hqk,khd->qhd", grad_score, keys, preferred_element_type=jnp.float32)
    rope_grad = jnp.einsum("hqk,kr->qhr", grad_score, rope_all, preferred_element_type=jnp.float32)
    stacked_left = jnp.stack([grad_score, prob_half], axis=0)
    stacked_right = jnp.stack(
        [jnp.transpose(queries, (1, 0, 2)), jnp.transpose(grad_out, (1, 0, 2))], axis=0
    )
    both = jnp.einsum(
        "ghqk,ghqd->ghkd", stacked_left, stacked_right, preferred_element_type=jnp.float32
    )
    radices = tuple(d[0] for d in reversed(gather_order(block_count)))
    both = both.reshape(both.shape[:2] + radices + (row_count, both.shape[3]))
    mine = scatter_relative(both, "blk", 2, jnp.bfloat16)
    mine = jnp.transpose(mine, (2, 0, 1, 3)).reshape(row_count, -1)
    flat = mine.astype(jnp.bfloat16)
    key_flat = flat[:, : head_count * D_NOPE]
    value_flat = flat[:, head_count * D_NOPE :]

    def back_project(grad_flat, weight):
        return lax.dot_general(
            grad_flat, weight, (((1,), (1,)), ((), ())), preferred_element_type=jnp.float32
        )

    latent_part = back_project(key_flat, w_uk) + back_project(value_flat, w_uv)
    sum_levels = digits_of(lax.axis_size("heads"))
    gather_levels = gather_order(block_count)
    comp_own = comp_all.reshape(radices + (row_count, col_width))[0]

    def own_products(flats):
        first_radix, first_stride = gather_levels[0]
        inner = list(reversed(gather_levels[1:-1]))
        slot_sums = []
        for slot in range(first_radix):
            left = comp_own[..., slot, :, :].reshape((-1, row_count, col_width))
            right = flats[..., slot, :, :].reshape((-1, row_count, flat.shape[1]))
            product = jnp.einsum("btl,btk->blk", left, right, preferred_element_type=jnp.float32)
            partial = product.astype(jnp.bfloat16).astype(jnp.float32)
            partial = partial.reshape(tuple(d[0] for d in inner) + partial.shape[1:])
            for radix, stride in inner:
                partial = ordered_sum([partial[k] for k in range(radix)], "blk", radix, stride)
            slot_sums.append(partial)
        return ordered_sum(slot_sums, "blk", first_radix, first_stride)

    latent_sum = latent_part
    flats = flat
    for level in range(max(len(sum_levels), len(gather_levels))):
        if level < len(gather_levels) - 1:
            flats = gather_step(flats, "blk", *gather_levels[level])
        elif level == len(gather_levels) - 1:
            flats = reduce_step(own_products(flats), "blk", *gather_levels[level], jnp.float32)
        if level < len(sum_levels):
            latent_sum = reduce_step(latent_sum, "heads", *sum_levels[level], jnp.bfloat16)
        flats, latent_sum = lax.optimization_barrier((flats, latent_sum))
    grad_latent = (latent_sum * factor).astype(jnp.bfloat16)
    weight_sum = flats
    weight_key_grad = weight_sum[:, : head_count * D_NOPE]
    weight_value_grad = weight_sum[:, head_count * D_NOPE :]

    grad_q_nope = query_grad.reshape(row_count, head_count * D_NOPE).astype(jnp.bfloat16)
    grad_q_rope = rope_grad.reshape(row_count, head_count * D_ROPE).astype(jnp.bfloat16)
    return (grad_q_nope, grad_q_rope, grad_latent, weight_key_grad, weight_value_grad)


def solution(mesh):
    in_specs = (
        P("blk", "heads"),
        P("blk", "heads"),
        P("blk", "heads"),
        P("blk", None),
        P(None, "blk"),
        P("blk"),
        P("blk"),
        P(None, "heads"),
        P(None, "heads"),
    )
    out_specs = (
        P("blk", "heads"),
        P("blk", "heads"),
        P("blk", None),
        P(None, "heads"),
        P(None, "heads"),
    )
    return jax.shard_map(body, mesh=mesh, in_specs=in_specs, out_specs=out_specs, check_vma=False)
```

```python
import jax
import jax.numpy as jnp
from jax import lax
from jax.sharding import PartitionSpec as P

D_ROPE = 64
D_NOPE = 128
D_V = 128
POS_SPLIT = 64


lowest = -1e30


def digits_of(size):
    found = []
    stride = 1
    rest = size
    for prime in (2, 3):
        if rest % prime == 0:
            found.append((prime, stride))
            stride *= prime
            rest //= prime
    while rest % 4 == 0:
        found.append((4, stride))
        stride *= 4
        rest //= 4
    prime = 2
    while rest > 1:
        while rest % prime == 0:
            found.append((prime, stride))
            stride *= prime
            rest //= prime
        prime += 1
    return found


def gather_order(size):
    return sorted(digits_of(size), key=lambda d: (d[0] != 3, -d[1]))


def digit_value(axis, radix, stride):
    return (lax.axis_index(axis) // stride) % radix


def shift_digit(x, axis, radix, stride, by):
    size = lax.axis_size(axis)
    pairs = []
    for i in range(size):
        r = (i // stride) % radix
        pairs.append((i, i + (((r + by) % radix) - r) * stride))
    return lax.ppermute(x, axis, pairs)


def ordered_pieces(own, axis, radix, stride):
    r = digit_value(axis, radix, stride)
    received = {by: shift_digit(own, axis, radix, stride, by) for by in range(1, radix)}
    return canonical(own, received, r, radix)


def canonical(own, received, r, radix):
    pieces = []
    for k in range(radix):
        piece = own
        for by in range(1, radix):
            piece = jnp.where((r - k) % radix == by, received[by], piece)
        pieces.append(piece)
    return pieces


def gather_step(buf, axis, radix, stride):
    received = [shift_digit(buf, axis, radix, stride, by) for by in range(1, radix)]
    pieces = [buf] + [received[radix - k - 1] for k in range(1, radix)]
    return jnp.stack(pieces, axis=0)


def gather_relative(block, axis):
    buf = block
    for radix, stride in gather_order(lax.axis_size(axis)):
        buf = gather_step(buf, axis, radix, stride)
    return buf


def scatter_relative(data, axis, lead, wire):
    for radix, stride in reversed(gather_order(lax.axis_size(axis))):
        head = (slice(None),) * lead
        total = data[head + (0,)]
        for by in range(1, radix):
            part = data[head + (by,)].astype(wire)
            total = total + shift_digit(part, axis, radix, stride, by).astype(jnp.float32)
        data = total
    return data


def ordered_sum(slots, axis, radix, stride):
    r = digit_value(axis, radix, stride)
    received = {by: slots[radix - by] for by in range(1, radix)}
    ordered = canonical(slots[0], received, r, radix)
    total = ordered[0]
    for piece in ordered[1:]:
        total = total + piece
    return total


def reduce_step(x, axis, radix, stride, wire):
    own = x.astype(wire)
    if radix == 2:
        return own.astype(jnp.float32) + shift_digit(own, axis, radix, stride, 1).astype(jnp.float32)
    pieces = ordered_pieces(own, axis, radix, stride)
    total = pieces[0].astype(jnp.float32)
    for piece in pieces[1:]:
        total = total + piece.astype(jnp.float32)
    return total


def body(q_nope, q_rope, d_out, latent, scale_exp, positions, spans, w_uk, w_uv):
    row_count = q_nope.shape[0]
    head_count = w_uk.shape[1] // D_NOPE
    col_width = latent.shape[1] - D_ROPE
    col_group = col_width // scale_exp.shape[0]
    block_count = lax.axis_size("blk")
    key_count = row_count * block_count
    soft_scale = (D_NOPE + D_ROPE) ** (-0.5)

    factor = jnp.exp2(jnp.repeat(jnp.transpose(scale_exp), col_group, axis=1).astype(jnp.float32))
    compressed = (latent[:, :col_width].astype(jnp.float32) * factor).astype(jnp.bfloat16)
    pos_hi = (positions // POS_SPLIT).astype(jnp.bfloat16)
    pos_lo = (positions % POS_SPLIT).astype(jnp.bfloat16)
    packed = jnp.concatenate(
        [compressed, latent[:, col_width:], pos_hi[:, None], pos_lo[:, None]], axis=1
    )
    everything = gather_relative(packed, "blk").reshape(key_count, packed.shape[1])
    comp_all = everything[:, :col_width]
    rope_all = everything[:, col_width : col_width + D_ROPE]
    key_pos = everything[:, col_width + D_ROPE].astype(jnp.int32) * POS_SPLIT + everything[
        :, col_width + D_ROPE + 1
    ].astype(jnp.int32)

    keys = jnp.dot(comp_all, w_uk, preferred_element_type=jnp.float32).astype(jnp.bfloat16)
    values = jnp.dot(comp_all, w_uv, preferred_element_type=jnp.float32).astype(jnp.bfloat16)
    keys = keys.reshape(key_count, head_count, D_NOPE)
    values = values.reshape(key_count, head_count, D_V)
    queries = q_nope.reshape(row_count, head_count, D_NOPE)
    query_rope = q_rope.reshape(row_count, head_count, D_ROPE)
    grad_out = d_out.reshape(row_count, head_count, D_V)

    scores = jnp.einsum("qhd,khd->hqk", queries, keys, preferred_element_type=jnp.float32)
    scores = scores + jnp.einsum(
        "qhr,kr->hqk", query_rope, rope_all, preferred_element_type=jnp.float32
    )
    scores = scores * soft_scale
    pairs = (key_pos[None, :] <= positions[:, None]) & (
        key_pos[None, :] >= positions[:, None] - spans[:, None]
    )
    masked = jnp.where(pairs[None], scores, lowest)
    row_max = jnp.max(masked, axis=2, keepdims=True)
    row_sum = jnp.sum(
        jnp.where(pairs[None], jnp.exp(masked - row_max), 0.0), axis=2, keepdims=True
    )
    log_norm = row_max + jnp.log(row_sum)
    prob_float = jnp.where(pairs[None], jnp.exp(scores - log_norm), 0.0)
    grad_prob = jnp.einsum("qhd,khd->hqk", grad_out, values, preferred_element_type=jnp.float32)
    delta_rows = jnp.sum(prob_float * grad_prob, axis=2, keepdims=True)
    grad_score = (prob_float * (grad_prob - delta_rows) * soft_scale).astype(jnp.bfloat16)
    prob_half = prob_float.astype(jnp.bfloat16)

    query_grad = jnp.einsum("hqk,khd->qhd", grad_score, keys, preferred_element_type=jnp.float32)
    rope_grad = jnp.einsum("hqk,kr->qhr", grad_score, rope_all, preferred_element_type=jnp.float32)
    stacked_left = jnp.stack([grad_score, prob_half], axis=0)
    stacked_right = jnp.stack(
        [jnp.transpose(queries, (1, 0, 2)), jnp.transpose(grad_out, (1, 0, 2))], axis=0
    )
    both = jnp.einsum(
        "ghqk,ghqd->ghkd", stacked_left, stacked_right, preferred_element_type=jnp.float32
    )
    radices = tuple(d[0] for d in reversed(gather_order(block_count)))
    both = both.reshape(both.shape[:2] + radices + (row_count, both.shape[3]))
    mine = scatter_relative(both, "blk", 2, jnp.bfloat16)
    mine = jnp.transpose(mine, (2, 0, 1, 3)).reshape(row_count, -1)
    flat = mine.astype(jnp.bfloat16)
    key_flat = flat[:, : head_count * D_NOPE]
    value_flat = flat[:, head_count * D_NOPE :]

    def back_project(grad_flat, weight):
        return lax.dot_general(
            grad_flat, weight, (((1,), (1,)), ((), ())), preferred_element_type=jnp.float32
        )

    latent_part = back_project(key_flat, w_uk) + back_project(value_flat, w_uv)
    sum_levels = digits_of(lax.axis_size("heads"))
    gather_levels = gather_order(block_count)
    comp_own = comp_all.reshape(radices + (row_count, col_width))[0]

    def own_products(flats):
        first_radix, first_stride = gather_levels[0]
        inner = list(reversed(gather_levels[1:-1]))
        slot_sums = []
        for slot in range(first_radix):
            left = comp_own[..., slot, :, :].reshape((-1, row_count, col_width))
            right = flats[..., slot, :, :].reshape((-1, row_count, flat.shape[1]))
            product = jnp.einsum("btl,btk->blk", left, right, preferred_element_type=jnp.float32)
            partial = product.astype(jnp.bfloat16).astype(jnp.float32)
            partial = partial.reshape(tuple(d[0] for d in inner) + partial.shape[1:])
            for radix, stride in inner:
                partial = ordered_sum([partial[k] for k in range(radix)], "blk", radix, stride)
            slot_sums.append(partial)
        return ordered_sum(slot_sums, "blk", first_radix, first_stride)

    latent_sum = latent_part
    flats = flat
    for level in range(max(len(sum_levels), len(gather_levels))):
        if level < len(gather_levels) - 1:
            flats = gather_step(flats, "blk", *gather_levels[level])
        elif level == len(gather_levels) - 1:
            flats = reduce_step(own_products(flats), "blk", *gather_levels[level], jnp.float32)
        if level < len(sum_levels):
            latent_sum = reduce_step(latent_sum, "heads", *sum_levels[level], jnp.bfloat16)
        flats, latent_sum = lax.optimization_barrier((flats, latent_sum))
    grad_latent = (latent_sum * factor).astype(jnp.bfloat16)
    weight_sum = flats
    weight_key_grad = weight_sum[:, : head_count * D_NOPE]
    weight_value_grad = weight_sum[:, head_count * D_NOPE :]

    grad_q_nope = query_grad.reshape(row_count, head_count * D_NOPE).astype(jnp.bfloat16)
    grad_q_rope = rope_grad.reshape(row_count, head_count * D_ROPE).astype(jnp.bfloat16)
    return (grad_q_nope, grad_q_rope, grad_latent, weight_key_grad, weight_value_grad)


def solution(mesh):
    in_specs = (
        P("blk", "heads"),
        P("blk", "heads"),
        P("blk", "heads"),
        P("blk", None),
        P(None, "blk"),
        P("blk"),
        P("blk"),
        P(None, "heads"),
        P(None, "heads"),
    )
    out_specs = (
        P("blk", "heads"),
        P("blk", "heads"),
        P("blk", None),
        P(None, "heads"),
        P(None, "heads"),
    )
    return jax.shard_map(body, mesh=mesh, in_specs=in_specs, out_specs=out_specs, check_vma=False)
```

```python
import jax
import jax.numpy as jnp
from jax import lax
from jax.sharding import PartitionSpec as P

D_ROPE = 64
D_NOPE = 128
D_V = 128
POS_SPLIT = 64
LANE = 128


lowest = -1e30


def digits_of(size):
    found = []
    stride = 1
    rest = size
    for prime in (2, 3):
        if rest % prime == 0:
            found.append((prime, stride))
            stride *= prime
            rest //= prime
    while rest % 4 == 0:
        found.append((4, stride))
        stride *= 4
        rest //= 4
    prime = 2
    while rest > 1:
        while rest % prime == 0:
            found.append((prime, stride))
            stride *= prime
            rest //= prime
        prime += 1
    return found


def gather_order(size):
    return sorted(digits_of(size), key=lambda d: (d[0] != 3, -d[1]))


def digit_value(axis, radix, stride):
    return (lax.axis_index(axis) // stride) % radix


def shift_digit(x, axis, radix, stride, by):
    size = lax.axis_size(axis)
    pairs = []
    for i in range(size):
        r = (i // stride) % radix
        pairs.append((i, i + (((r + by) % radix) - r) * stride))
    return lax.ppermute(x, axis, pairs)


def ordered_pieces(own, axis, radix, stride):
    r = digit_value(axis, radix, stride)
    received = {by: shift_digit(own, axis, radix, stride, by) for by in range(1, radix)}
    return canonical(own, received, r, radix)


def canonical(own, received, r, radix):
    pieces = []
    for k in range(radix):
        piece = own
        for by in range(1, radix):
            piece = jnp.where((r - k) % radix == by, received[by], piece)
        pieces.append(piece)
    return pieces


def gather_step(buf, axis, radix, stride):
    received = [shift_digit(buf, axis, radix, stride, by) for by in range(1, radix)]
    pieces = [buf] + [received[radix - k - 1] for k in range(1, radix)]
    return jnp.stack(pieces, axis=0)


def gather_relative(block, axis):
    buf = block
    levels = gather_order(lax.axis_size(axis))
    for radix, stride in levels[:-1]:
        buf = gather_step(buf, axis, radix, stride)
    width = buf.shape[-1]
    lanes = -(-width // LANE) * LANE
    padded = jnp.pad(buf, [(0, 0)] * (buf.ndim - 1) + [(0, lanes - width)])
    return gather_step(padded, axis, *levels[-1])[..., :width]


def scatter_relative(data, axis, lead, wire):
    for radix, stride in reversed(gather_order(lax.axis_size(axis))):
        head = (slice(None),) * lead
        total = data[head + (0,)]
        for by in range(1, radix):
            part = data[head + (by,)].astype(wire)
            total = total + shift_digit(part, axis, radix, stride, by).astype(jnp.float32)
        data = total
    return data


def ordered_sum(slots, axis, radix, stride):
    r = digit_value(axis, radix, stride)
    received = {by: slots[radix - by] for by in range(1, radix)}
    ordered = canonical(slots[0], received, r, radix)
    total = ordered[0]
    for piece in ordered[1:]:
        total = total + piece
    return total


def reduce_step(x, axis, radix, stride, wire):
    own = x.astype(wire)
    if radix == 2:
        return own.astype(jnp.float32) + shift_digit(own, axis, radix, stride, 1).astype(jnp.float32)
    pieces = ordered_pieces(own, axis, radix, stride)
    total = pieces[0].astype(jnp.float32)
    for piece in pieces[1:]:
        total = total + piece.astype(jnp.float32)
    return total


def body(q_nope, q_rope, d_out, latent, scale_exp, positions, spans, w_uk, w_uv):
    row_count = q_nope.shape[0]
    head_count = w_uk.shape[1] // D_NOPE
    col_width = latent.shape[1] - D_ROPE
    col_group = col_width // scale_exp.shape[0]
    block_count = lax.axis_size("blk")
    key_count = row_count * block_count
    soft_scale = (D_NOPE + D_ROPE) ** (-0.5)

    factor = jnp.exp2(jnp.repeat(jnp.transpose(scale_exp), col_group, axis=1).astype(jnp.float32))
    compressed = (latent[:, :col_width].astype(jnp.float32) * factor).astype(jnp.bfloat16)
    pos_hi = (positions // POS_SPLIT).astype(jnp.bfloat16)
    pos_lo = (positions % POS_SPLIT).astype(jnp.bfloat16)
    packed = jnp.concatenate(
        [compressed, latent[:, col_width:], pos_hi[:, None], pos_lo[:, None]], axis=1
    )
    everything = gather_relative(packed, "blk").reshape(key_count, packed.shape[1])
    comp_all = everything[:, :col_width]
    rope_all = everything[:, col_width : col_width + D_ROPE]
    key_pos = everything[:, col_width + D_ROPE].astype(jnp.int32) * POS_SPLIT + everything[
        :, col_width + D_ROPE + 1
    ].astype(jnp.int32)

    keys = jnp.dot(comp_all, w_uk, preferred_element_type=jnp.float32).astype(jnp.bfloat16)
    values = jnp.dot(comp_all, w_uv, preferred_element_type=jnp.float32).astype(jnp.bfloat16)
    keys = keys.reshape(key_count, head_count, D_NOPE)
    values = values.reshape(key_count, head_count, D_V)
    queries = q_nope.reshape(row_count, head_count, D_NOPE)
    query_rope = q_rope.reshape(row_count, head_count, D_ROPE)
    grad_out = d_out.reshape(row_count, head_count, D_V)

    scores = jnp.einsum("qhd,khd->hqk", queries, keys, preferred_element_type=jnp.float32)
    scores = scores + jnp.einsum(
        "qhr,kr->hqk", query_rope, rope_all, preferred_element_type=jnp.float32
    )
    scores = scores * soft_scale
    pairs = (key_pos[None, :] <= positions[:, None]) & (
        key_pos[None, :] >= positions[:, None] - spans[:, None]
    )
    masked = jnp.where(pairs[None], scores, lowest)
    row_max = jnp.max(masked, axis=2, keepdims=True)
    row_sum = jnp.sum(
        jnp.where(pairs[None], jnp.exp(masked - row_max), 0.0), axis=2, keepdims=True
    )
    log_norm = row_max + jnp.log(row_sum)
    prob_float = jnp.where(pairs[None], jnp.exp(scores - log_norm), 0.0)
    grad_prob = jnp.einsum("qhd,khd->hqk", grad_out, values, preferred_element_type=jnp.float32)
    delta_rows = jnp.sum(prob_float * grad_prob, axis=2, keepdims=True)
    grad_score = (prob_float * (grad_prob - delta_rows) * soft_scale).astype(jnp.bfloat16)
    prob_half = prob_float.astype(jnp.bfloat16)

    query_grad = jnp.einsum("hqk,khd->qhd", grad_score, keys, preferred_element_type=jnp.float32)
    rope_grad = jnp.einsum("hqk,kr->qhr", grad_score, rope_all, preferred_element_type=jnp.float32)
    stacked_left = jnp.stack([grad_score, prob_half], axis=0)
    stacked_right = jnp.stack(
        [jnp.transpose(queries, (1, 0, 2)), jnp.transpose(grad_out, (1, 0, 2))], axis=0
    )
    both = jnp.einsum(
        "ghqk,ghqd->ghkd", stacked_left, stacked_right, preferred_element_type=jnp.float32
    )
    radices = tuple(d[0] for d in reversed(gather_order(block_count)))
    both = both.reshape(both.shape[:2] + radices + (row_count, both.shape[3]))
    mine = scatter_relative(both, "blk", 2, jnp.bfloat16)
    mine = jnp.transpose(mine, (2, 0, 1, 3)).reshape(row_count, -1)
    flat = mine.astype(jnp.bfloat16)
    key_flat = flat[:, : head_count * D_NOPE]
    value_flat = flat[:, head_count * D_NOPE :]

    def back_project(grad_flat, weight):
        return lax.dot_general(
            grad_flat, weight, (((1,), (1,)), ((), ())), preferred_element_type=jnp.float32
        )

    latent_part = back_project(key_flat, w_uk) + back_project(value_flat, w_uv)
    sum_levels = digits_of(lax.axis_size("heads"))
    gather_levels = gather_order(block_count)
    comp_own = comp_all.reshape(radices + (row_count, col_width))[0]

    def own_products(flats):
        first_radix, first_stride = gather_levels[0]
        inner = list(reversed(gather_levels[1:-1]))
        slot_sums = []
        for slot in range(first_radix):
            left = comp_own[..., slot, :, :].reshape((-1, row_count, col_width))
            right = flats[..., slot, :, :].reshape((-1, row_count, flat.shape[1]))
            product = jnp.einsum("btl,btk->blk", left, right, preferred_element_type=jnp.float32)
            partial = product.astype(jnp.bfloat16).astype(jnp.float32)
            partial = partial.reshape(tuple(d[0] for d in inner) + partial.shape[1:])
            for radix, stride in inner:
                partial = ordered_sum([partial[k] for k in range(radix)], "blk", radix, stride)
            slot_sums.append(partial)
        return ordered_sum(slot_sums, "blk", first_radix, first_stride)

    latent_sum = latent_part
    flats = flat
    for level in range(max(len(sum_levels), len(gather_levels))):
        if level < len(gather_levels) - 1:
            flats = gather_step(flats, "blk", *gather_levels[level])
        elif level == len(gather_levels) - 1:
            flats = reduce_step(own_products(flats), "blk", *gather_levels[level], jnp.float32)
        if level < len(sum_levels):
            latent_sum = reduce_step(latent_sum, "heads", *sum_levels[level], jnp.bfloat16)
        flats, latent_sum = lax.optimization_barrier((flats, latent_sum))
    grad_latent = (latent_sum * factor).astype(jnp.bfloat16)
    weight_sum = flats
    weight_key_grad = weight_sum[:, : head_count * D_NOPE]
    weight_value_grad = weight_sum[:, head_count * D_NOPE :]

    grad_q_nope = query_grad.reshape(row_count, head_count * D_NOPE).astype(jnp.bfloat16)
    grad_q_rope = rope_grad.reshape(row_count, head_count * D_ROPE).astype(jnp.bfloat16)
    return (grad_q_nope, grad_q_rope, grad_latent, weight_key_grad, weight_value_grad)


def solution(mesh):
    in_specs = (
        P("blk", "heads"),
        P("blk", "heads"),
        P("blk", "heads"),
        P("blk", None),
        P(None, "blk"),
        P("blk"),
        P("blk"),
        P(None, "heads"),
        P(None, "heads"),
    )
    out_specs = (
        P("blk", "heads"),
        P("blk", "heads"),
        P("blk", None),
        P(None, "heads"),
        P(None, "heads"),
    )
    return jax.shard_map(body, mesh=mesh, in_specs=in_specs, out_specs=out_specs, check_vma=False)
```

```python
import jax
import jax.numpy as jnp
from jax import lax
from jax.sharding import PartitionSpec as P

D_ROPE = 64
D_NOPE = 128
D_V = 128
POS_SPLIT = 64
LANE = 128


lowest = -1e30


def digits_of(size):
    found = []
    stride = 1
    rest = size
    for prime in (2, 3):
        if rest % prime == 0:
            found.append((prime, stride))
            stride *= prime
            rest //= prime
    while rest % 4 == 0:
        found.append((4, stride))
        stride *= 4
        rest //= 4
    prime = 2
    while rest > 1:
        while rest % prime == 0:
            found.append((prime, stride))
            stride *= prime
            rest //= prime
        prime += 1
    return found


def gather_order(size):
    return sorted(digits_of(size), key=lambda d: (d[0] != 3, -d[1]))


def digit_value(axis, radix, stride):
    return (lax.axis_index(axis) // stride) % radix


def shift_digit(x, axis, radix, stride, by):
    size = lax.axis_size(axis)
    pairs = []
    for i in range(size):
        r = (i // stride) % radix
        pairs.append((i, i + (((r + by) % radix) - r) * stride))
    return lax.ppermute(x, axis, pairs)


def ordered_pieces(own, axis, radix, stride):
    r = digit_value(axis, radix, stride)
    received = {by: shift_digit(own, axis, radix, stride, by) for by in range(1, radix)}
    return canonical(own, received, r, radix)


def canonical(own, received, r, radix):
    pieces = []
    for k in range(radix):
        piece = own
        for by in range(1, radix):
            piece = jnp.where((r - k) % radix == by, received[by], piece)
        pieces.append(piece)
    return pieces


def gather_step(buf, axis, radix, stride):
    received = [shift_digit(buf, axis, radix, stride, by) for by in range(1, radix)]
    pieces = [buf] + [received[radix - k - 1] for k in range(1, radix)]
    return jnp.stack(pieces, axis=0)


def gather_relative(block, axis):
    buf = block
    levels = gather_order(lax.axis_size(axis))
    for radix, stride in levels[:-1]:
        buf = gather_step(buf, axis, radix, stride)
    width = buf.shape[-1]
    lanes = -(-width // LANE) * LANE
    padded = jnp.pad(buf, [(0, 0)] * (buf.ndim - 1) + [(0, lanes - width)])
    return gather_step(padded, axis, *levels[-1])[..., :width]


def scatter_relative(data, axis, lead, wire):
    for radix, stride in reversed(gather_order(lax.axis_size(axis))):
        head = (slice(None),) * lead
        total = data[head + (0,)]
        for by in range(1, radix):
            part = data[head + (by,)].astype(wire)
            total = total + shift_digit(part, axis, radix, stride, by).astype(jnp.float32)
        data = total
    return data


def ordered_sum(slots, axis, radix, stride):
    r = digit_value(axis, radix, stride)
    received = {by: slots[radix - by] for by in range(1, radix)}
    ordered = canonical(slots[0], received, r, radix)
    total = ordered[0]
    for piece in ordered[1:]:
        total = total + piece
    return total


def reduce_step(x, axis, radix, stride, wire):
    own = x.astype(wire)
    if radix == 2:
        return own.astype(jnp.float32) + shift_digit(own, axis, radix, stride, 1).astype(jnp.float32)
    pieces = ordered_pieces(own, axis, radix, stride)
    total = pieces[0].astype(jnp.float32)
    for piece in pieces[1:]:
        total = total + piece.astype(jnp.float32)
    return total


def body(q_nope, q_rope, d_out, latent, scale_exp, positions, spans, w_uk, w_uv):
    row_count = q_nope.shape[0]
    head_count = w_uk.shape[1] // D_NOPE
    col_width = latent.shape[1] - D_ROPE
    col_group = col_width // scale_exp.shape[0]
    block_count = lax.axis_size("blk")
    key_count = row_count * block_count
    soft_scale = (D_NOPE + D_ROPE) ** (-0.5)

    factor = jnp.exp2(jnp.repeat(jnp.transpose(scale_exp), col_group, axis=1).astype(jnp.float32))
    compressed = (latent[:, :col_width].astype(jnp.float32) * factor).astype(jnp.bfloat16)
    pos_hi = (positions // POS_SPLIT).astype(jnp.bfloat16)
    pos_lo = (positions % POS_SPLIT).astype(jnp.bfloat16)
    used = col_width + D_ROPE + 2
    spare = jnp.zeros((row_count, -(-used // LANE) * LANE - used), jnp.bfloat16)
    packed = jnp.concatenate(
        [compressed, latent[:, col_width:], pos_hi[:, None], pos_lo[:, None], spare], axis=1
    )
    everything = gather_relative(packed, "blk").reshape(key_count, packed.shape[1])
    comp_all = everything[:, :col_width]
    rope_all = everything[:, col_width : col_width + D_ROPE]
    key_pos = everything[:, col_width + D_ROPE].astype(jnp.int32) * POS_SPLIT + everything[
        :, col_width + D_ROPE + 1
    ].astype(jnp.int32)

    keys = jnp.dot(comp_all, w_uk, preferred_element_type=jnp.float32).astype(jnp.bfloat16)
    values = jnp.dot(comp_all, w_uv, preferred_element_type=jnp.float32).astype(jnp.bfloat16)
    keys = keys.reshape(key_count, head_count, D_NOPE)
    values = values.reshape(key_count, head_count, D_V)
    queries = q_nope.reshape(row_count, head_count, D_NOPE)
    query_rope = q_rope.reshape(row_count, head_count, D_ROPE)
    grad_out = d_out.reshape(row_count, head_count, D_V)

    scores = jnp.einsum("qhd,khd->hqk", queries, keys, preferred_element_type=jnp.float32)
    scores = scores + jnp.einsum(
        "qhr,kr->hqk", query_rope, rope_all, preferred_element_type=jnp.float32
    )
    scores = scores * soft_scale
    pairs = (key_pos[None, :] <= positions[:, None]) & (
        key_pos[None, :] >= positions[:, None] - spans[:, None]
    )
    masked = jnp.where(pairs[None], scores, lowest)
    row_max = jnp.max(masked, axis=2, keepdims=True)
    row_sum = jnp.sum(
        jnp.where(pairs[None], jnp.exp(masked - row_max), 0.0), axis=2, keepdims=True
    )
    log_norm = row_max + jnp.log(row_sum)
    prob_float = jnp.where(pairs[None], jnp.exp(scores - log_norm), 0.0)
    grad_prob = jnp.einsum("qhd,khd->hqk", grad_out, values, preferred_element_type=jnp.float32)
    delta_rows = jnp.sum(prob_float * grad_prob, axis=2, keepdims=True)
    grad_score = (prob_float * (grad_prob - delta_rows) * soft_scale).astype(jnp.bfloat16)
    prob_half = prob_float.astype(jnp.bfloat16)

    query_grad = jnp.einsum("hqk,khd->qhd", grad_score, keys, preferred_element_type=jnp.float32)
    rope_grad = jnp.einsum("hqk,kr->qhr", grad_score, rope_all, preferred_element_type=jnp.float32)
    stacked_left = jnp.stack([grad_score, prob_half], axis=0)
    stacked_right = jnp.stack(
        [jnp.transpose(queries, (1, 0, 2)), jnp.transpose(grad_out, (1, 0, 2))], axis=0
    )
    both = jnp.einsum(
        "ghqk,ghqd->ghkd", stacked_left, stacked_right, preferred_element_type=jnp.float32
    )
    radices = tuple(d[0] for d in reversed(gather_order(block_count)))
    both = both.reshape(both.shape[:2] + radices + (row_count, both.shape[3]))
    mine = scatter_relative(both, "blk", 2, jnp.bfloat16)
    mine = jnp.transpose(mine, (2, 0, 1, 3)).reshape(row_count, -1)
    flat = mine.astype(jnp.bfloat16)
    key_flat = flat[:, : head_count * D_NOPE]
    value_flat = flat[:, head_count * D_NOPE :]

    def back_project(grad_flat, weight):
        return lax.dot_general(
            grad_flat, weight, (((1,), (1,)), ((), ())), preferred_element_type=jnp.float32
        )

    latent_part = back_project(key_flat, w_uk) + back_project(value_flat, w_uv)
    sum_levels = digits_of(lax.axis_size("heads"))
    gather_levels = gather_order(block_count)
    comp_own = comp_all.reshape(radices + (row_count, col_width))[0]

    def own_products(flats):
        first_radix, first_stride = gather_levels[0]
        inner = list(reversed(gather_levels[1:-1]))
        slot_sums = []
        for slot in range(first_radix):
            left = comp_own[..., slot, :, :].reshape((-1, row_count, col_width))
            right = flats[..., slot, :, :].reshape((-1, row_count, flat.shape[1]))
            product = jnp.einsum("btl,btk->blk", left, right, preferred_element_type=jnp.float32)
            partial = product.astype(jnp.bfloat16).astype(jnp.float32)
            partial = partial.reshape(tuple(d[0] for d in inner) + partial.shape[1:])
            for radix, stride in inner:
                partial = ordered_sum([partial[k] for k in range(radix)], "blk", radix, stride)
            slot_sums.append(partial)
        return ordered_sum(slot_sums, "blk", first_radix, first_stride)

    latent_sum = latent_part
    flats = flat
    for level in range(max(len(sum_levels), len(gather_levels))):
        if level < len(gather_levels) - 1:
            flats = gather_step(flats, "blk", *gather_levels[level])
        elif level == len(gather_levels) - 1:
            flats = reduce_step(own_products(flats), "blk", *gather_levels[level], jnp.float32)
        if level < len(sum_levels):
            latent_sum = reduce_step(latent_sum, "heads", *sum_levels[level], jnp.bfloat16)
        flats, latent_sum = lax.optimization_barrier((flats, latent_sum))
    grad_latent = (latent_sum * factor).astype(jnp.bfloat16)
    weight_sum = flats
    weight_key_grad = weight_sum[:, : head_count * D_NOPE]
    weight_value_grad = weight_sum[:, head_count * D_NOPE :]

    grad_q_nope = query_grad.reshape(row_count, head_count * D_NOPE).astype(jnp.bfloat16)
    grad_q_rope = rope_grad.reshape(row_count, head_count * D_ROPE).astype(jnp.bfloat16)
    return (grad_q_nope, grad_q_rope, grad_latent, weight_key_grad, weight_value_grad)


def solution(mesh):
    in_specs = (
        P("blk", "heads"),
        P("blk", "heads"),
        P("blk", "heads"),
        P("blk", None),
        P(None, "blk"),
        P("blk"),
        P("blk"),
        P(None, "heads"),
        P(None, "heads"),
    )
    out_specs = (
        P("blk", "heads"),
        P("blk", "heads"),
        P("blk", None),
        P(None, "heads"),
        P(None, "heads"),
    )
    return jax.shard_map(body, mesh=mesh, in_specs=in_specs, out_specs=out_specs, check_vma=False)
```

```python
import jax
import jax.numpy as jnp
from jax import lax
from jax.sharding import PartitionSpec as P

D_ROPE = 64
D_NOPE = 128
D_V = 128
POS_SPLIT = 64
LANE = 128


lowest = -1e30


def digits_of(size):
    found = []
    stride = 1
    rest = size
    for prime in (2, 3):
        if rest % prime == 0:
            found.append((prime, stride))
            stride *= prime
            rest //= prime
    while rest % 4 == 0:
        found.append((4, stride))
        stride *= 4
        rest //= 4
    prime = 2
    while rest > 1:
        while rest % prime == 0:
            found.append((prime, stride))
            stride *= prime
            rest //= prime
        prime += 1
    return found


def gather_order(size):
    return sorted(digits_of(size), key=lambda d: (d[0] != 3, -d[1]))


def digit_value(axis, radix, stride):
    return (lax.axis_index(axis) // stride) % radix


def shift_digit(x, axis, radix, stride, by):
    size = lax.axis_size(axis)
    pairs = []
    for i in range(size):
        r = (i // stride) % radix
        pairs.append((i, i + (((r + by) % radix) - r) * stride))
    return lax.ppermute(x, axis, pairs)


def ordered_pieces(own, axis, radix, stride):
    r = digit_value(axis, radix, stride)
    received = {by: shift_digit(own, axis, radix, stride, by) for by in range(1, radix)}
    return canonical(own, received, r, radix)


def canonical(own, received, r, radix):
    pieces = []
    for k in range(radix):
        piece = own
        for by in range(1, radix):
            piece = jnp.where((r - k) % radix == by, received[by], piece)
        pieces.append(piece)
    return pieces


def gather_step(buf, axis, radix, stride):
    received = [shift_digit(buf, axis, radix, stride, by) for by in range(1, radix)]
    pieces = [buf] + [received[radix - k - 1] for k in range(1, radix)]
    return jnp.stack(pieces, axis=0)


def gather_relative(block, axis):
    buf = block
    levels = gather_order(lax.axis_size(axis))
    for radix, stride in levels[:-1]:
        buf = gather_step(buf, axis, radix, stride)
    width = buf.shape[-1]
    lanes = -(-width // LANE) * LANE
    padded = jnp.pad(buf, [(0, 0)] * (buf.ndim - 1) + [(0, lanes - width)])
    return gather_step(padded, axis, *levels[-1])[..., :width]


def scatter_relative(data, axis, lead, wire):
    for radix, stride in reversed(gather_order(lax.axis_size(axis))):
        head = (slice(None),) * lead
        total = data[head + (0,)]
        for by in range(1, radix):
            part = data[head + (by,)].astype(wire)
            total = total + shift_digit(part, axis, radix, stride, by).astype(jnp.float32)
        data = total
    return data


def ordered_sum(slots, axis, radix, stride):
    r = digit_value(axis, radix, stride)
    received = {by: slots[radix - by] for by in range(1, radix)}
    ordered = canonical(slots[0], received, r, radix)
    total = ordered[0]
    for piece in ordered[1:]:
        total = total + piece
    return total


def reduce_step(x, axis, radix, stride, wire):
    own = x.astype(wire)
    if radix == 2:
        return own.astype(jnp.float32) + shift_digit(own, axis, radix, stride, 1).astype(jnp.float32)
    pieces = ordered_pieces(own, axis, radix, stride)
    total = pieces[0].astype(jnp.float32)
    for piece in pieces[1:]:
        total = total + piece.astype(jnp.float32)
    return total


def body(q_nope, q_rope, d_out, latent, scale_exp, positions, spans, w_uk, w_uv):
    row_count = q_nope.shape[0]
    head_count = w_uk.shape[1] // D_NOPE
    col_width = latent.shape[1] - D_ROPE
    col_group = col_width // scale_exp.shape[0]
    block_count = lax.axis_size("blk")
    key_count = row_count * block_count
    soft_scale = (D_NOPE + D_ROPE) ** (-0.5)

    factor = jnp.exp2(jnp.repeat(jnp.transpose(scale_exp), col_group, axis=1).astype(jnp.float32))
    compressed = (latent[:, :col_width].astype(jnp.float32) * factor).astype(jnp.bfloat16)
    pos_hi = (positions // POS_SPLIT).astype(jnp.bfloat16)
    pos_lo = (positions % POS_SPLIT).astype(jnp.bfloat16)
    packed = jnp.concatenate(
        [compressed, latent[:, col_width:], pos_hi[:, None], pos_lo[:, None]], axis=1
    )
    everything = gather_relative(packed, "blk").reshape(key_count, packed.shape[1])
    comp_all = everything[:, :col_width]
    rope_all = everything[:, col_width : col_width + D_ROPE]
    key_pos = everything[:, col_width + D_ROPE].astype(jnp.int32) * POS_SPLIT + everything[
        :, col_width + D_ROPE + 1
    ].astype(jnp.int32)

    keys = jnp.dot(comp_all, w_uk, preferred_element_type=jnp.float32).astype(jnp.bfloat16)
    values = jnp.dot(comp_all, w_uv, preferred_element_type=jnp.float32).astype(jnp.bfloat16)
    keys = keys.reshape(key_count, head_count, D_NOPE)
    values = values.reshape(key_count, head_count, D_V)
    queries = q_nope.reshape(row_count, head_count, D_NOPE)
    query_rope = q_rope.reshape(row_count, head_count, D_ROPE)
    grad_out = d_out.reshape(row_count, head_count, D_V)

    scores = jnp.einsum("qhd,khd->hqk", queries, keys, preferred_element_type=jnp.float32)
    scores = scores + jnp.einsum(
        "qhr,kr->hqk", query_rope, rope_all, preferred_element_type=jnp.float32
    )
    scores = scores * soft_scale
    pairs = (key_pos[None, :] <= positions[:, None]) & (
        key_pos[None, :] >= positions[:, None] - spans[:, None]
    )
    masked = jnp.where(pairs[None], scores, lowest)
    row_max = jnp.max(masked, axis=2, keepdims=True)
    row_sum = jnp.sum(
        jnp.where(pairs[None], jnp.exp(masked - row_max), 0.0), axis=2, keepdims=True
    )
    log_norm = row_max + jnp.log(row_sum)
    prob_float = jnp.where(pairs[None], jnp.exp(scores - log_norm), 0.0)
    grad_prob = jnp.einsum("qhd,khd->hqk", grad_out, values, preferred_element_type=jnp.float32)
    delta_rows = jnp.sum(prob_float * grad_prob, axis=2, keepdims=True)
    grad_score = (prob_float * (grad_prob - delta_rows) * soft_scale).astype(jnp.bfloat16)
    prob_half = prob_float.astype(jnp.bfloat16)

    query_grad = jnp.einsum("hqk,khd->qhd", grad_score, keys, preferred_element_type=jnp.float32)
    rope_grad = jnp.einsum("hqk,kr->qhr", grad_score, rope_all, preferred_element_type=jnp.float32)
    stacked_left = jnp.stack([grad_score, prob_half], axis=0)
    stacked_right = jnp.stack(
        [jnp.transpose(queries, (1, 0, 2)), jnp.transpose(grad_out, (1, 0, 2))], axis=0
    )
    both = jnp.einsum(
        "ghqk,ghqd->ghkd", stacked_left, stacked_right, preferred_element_type=jnp.float32
    )
    radices = tuple(d[0] for d in reversed(gather_order(block_count)))
    both = both.reshape(both.shape[:2] + radices + (row_count, both.shape[3]))
    mine = scatter_relative(both, "blk", 2, jnp.bfloat16)
    mine = jnp.transpose(mine, (2, 0, 1, 3)).reshape(row_count, -1)
    flat = mine.astype(jnp.bfloat16)
    key_flat = flat[:, : head_count * D_NOPE]
    value_flat = flat[:, head_count * D_NOPE :]

    def back_project(grad_flat, weight):
        return lax.dot_general(
            grad_flat, weight, (((1,), (1,)), ((), ())), preferred_element_type=jnp.float32
        )

    latent_part = back_project(key_flat, w_uk) + back_project(value_flat, w_uv)
    sum_levels = digits_of(lax.axis_size("heads"))
    if len(sum_levels) > 2 and sum_levels[-1][0] == 4:
        last_stride = sum_levels[-1][1]
        sum_levels = sum_levels[:-1] + [(2, last_stride), (2, last_stride * 2)]
    gather_levels = gather_order(block_count)
    comp_own = comp_all.reshape(radices + (row_count, col_width))[0]

    def own_products(flats):
        first_radix, first_stride = gather_levels[0]
        inner = list(reversed(gather_levels[1:-1]))
        slot_sums = []
        for slot in range(first_radix):
            left = comp_own[..., slot, :, :].reshape((-1, row_count, col_width))
            right = flats[..., slot, :, :].reshape((-1, row_count, flat.shape[1]))
            product = jnp.einsum("btl,btk->blk", left, right, preferred_element_type=jnp.float32)
            partial = product.astype(jnp.bfloat16).astype(jnp.float32)
            partial = partial.reshape(tuple(d[0] for d in inner) + partial.shape[1:])
            for radix, stride in inner:
                partial = ordered_sum([partial[k] for k in range(radix)], "blk", radix, stride)
            slot_sums.append(partial)
        return ordered_sum(slot_sums, "blk", first_radix, first_stride)

    latent_sum = latent_part
    flats = flat
    for level in range(max(len(sum_levels), len(gather_levels))):
        if level < len(gather_levels) - 1:
            flats = gather_step(flats, "blk", *gather_levels[level])
        elif level == len(gather_levels) - 1:
            flats = reduce_step(own_products(flats), "blk", *gather_levels[level], jnp.float32)
        if level < len(sum_levels):
            latent_sum = reduce_step(latent_sum, "heads", *sum_levels[level], jnp.bfloat16)
        flats, latent_sum = lax.optimization_barrier((flats, latent_sum))
    grad_latent = (latent_sum * factor).astype(jnp.bfloat16)
    weight_sum = flats
    weight_key_grad = weight_sum[:, : head_count * D_NOPE]
    weight_value_grad = weight_sum[:, head_count * D_NOPE :]

    grad_q_nope = query_grad.reshape(row_count, head_count * D_NOPE).astype(jnp.bfloat16)
    grad_q_rope = rope_grad.reshape(row_count, head_count * D_ROPE).astype(jnp.bfloat16)
    return (grad_q_nope, grad_q_rope, grad_latent, weight_key_grad, weight_value_grad)


def solution(mesh):
    in_specs = (
        P("blk", "heads"),
        P("blk", "heads"),
        P("blk", "heads"),
        P("blk", None),
        P(None, "blk"),
        P("blk"),
        P("blk"),
        P(None, "heads"),
        P(None, "heads"),
    )
    out_specs = (
        P("blk", "heads"),
        P("blk", "heads"),
        P("blk", None),
        P(None, "heads"),
        P(None, "heads"),
    )
    return jax.shard_map(body, mesh=mesh, in_specs=in_specs, out_specs=out_specs, check_vma=False)
```

```python
import jax
import jax.numpy as jnp
from jax import lax
from jax.sharding import PartitionSpec as P

D_ROPE = 64
D_NOPE = 128
D_V = 128
POS_SPLIT = 64
LANE = 128


lowest = -1e30


def digits_of(size):
    found = []
    stride = 1
    rest = size
    for prime in (2, 3):
        if rest % prime == 0:
            found.append((prime, stride))
            stride *= prime
            rest //= prime
    while rest % 4 == 0:
        found.append((4, stride))
        stride *= 4
        rest //= 4
    prime = 2
    while rest > 1:
        while rest % prime == 0:
            found.append((prime, stride))
            stride *= prime
            rest //= prime
        prime += 1
    return found


def gather_order(size):
    return sorted(digits_of(size), key=lambda d: (d[0] != 3, -d[1]))


def digit_value(axis, radix, stride):
    return (lax.axis_index(axis) // stride) % radix


def shift_digit(x, axis, radix, stride, by):
    size = lax.axis_size(axis)
    pairs = []
    for i in range(size):
        r = (i // stride) % radix
        pairs.append((i, i + (((r + by) % radix) - r) * stride))
    return lax.ppermute(x, axis, pairs)


def ordered_pieces(own, axis, radix, stride):
    r = digit_value(axis, radix, stride)
    received = {by: shift_digit(own, axis, radix, stride, by) for by in range(1, radix)}
    return canonical(own, received, r, radix)


def canonical(own, received, r, radix):
    pieces = []
    for k in range(radix):
        piece = own
        for by in range(1, radix):
            piece = jnp.where((r - k) % radix == by, received[by], piece)
        pieces.append(piece)
    return pieces


def gather_step(buf, axis, radix, stride):
    received = [shift_digit(buf, axis, radix, stride, by) for by in range(1, radix)]
    pieces = [buf] + [received[radix - k - 1] for k in range(1, radix)]
    return jnp.stack(pieces, axis=0)


def gather_relative(block, axis):
    buf = block
    levels = gather_order(lax.axis_size(axis))
    for radix, stride in levels[:-1]:
        buf = gather_step(buf, axis, radix, stride)
    width = buf.shape[-1]
    lanes = -(-width // LANE) * LANE
    padded = jnp.pad(buf, [(0, 0)] * (buf.ndim - 1) + [(0, lanes - width)])
    return gather_step(padded, axis, *levels[-1])[..., :width]


def scatter_relative(data, axis, lead, wire):
    for radix, stride in reversed(gather_order(lax.axis_size(axis))):
        head = (slice(None),) * lead
        total = data[head + (0,)]
        for by in range(1, radix):
            part = data[head + (by,)].astype(wire)
            total = total + shift_digit(part, axis, radix, stride, by).astype(jnp.float32)
        data = total
    return data


def ordered_sum(slots, axis, radix, stride):
    r = digit_value(axis, radix, stride)
    received = {by: slots[radix - by] for by in range(1, radix)}
    ordered = canonical(slots[0], received, r, radix)
    total = ordered[0]
    for piece in ordered[1:]:
        total = total + piece
    return total


def reduce_step(x, axis, radix, stride, wire):
    own = x.astype(wire)
    if radix == 2:
        return own.astype(jnp.float32) + shift_digit(own, axis, radix, stride, 1).astype(jnp.float32)
    pieces = ordered_pieces(own, axis, radix, stride)
    total = pieces[0].astype(jnp.float32)
    for piece in pieces[1:]:
        total = total + piece.astype(jnp.float32)
    return total


def body(q_nope, q_rope, d_out, latent, scale_exp, positions, spans, w_uk, w_uv):
    row_count = q_nope.shape[0]
    head_count = w_uk.shape[1] // D_NOPE
    col_width = latent.shape[1] - D_ROPE
    col_group = col_width // scale_exp.shape[0]
    block_count = lax.axis_size("blk")
    key_count = row_count * block_count
    soft_scale = (D_NOPE + D_ROPE) ** (-0.5)

    factor = jnp.exp2(jnp.repeat(jnp.transpose(scale_exp), col_group, axis=1).astype(jnp.float32))
    compressed = (latent[:, :col_width].astype(jnp.float32) * factor).astype(jnp.bfloat16)
    pos_hi = (positions // POS_SPLIT).astype(jnp.bfloat16)
    pos_lo = (positions % POS_SPLIT).astype(jnp.bfloat16)
    packed = jnp.concatenate(
        [compressed, latent[:, col_width:], pos_hi[:, None], pos_lo[:, None]], axis=1
    )
    everything = gather_relative(packed, "blk").reshape(key_count, packed.shape[1])
    comp_all = everything[:, :col_width]
    rope_all = everything[:, col_width : col_width + D_ROPE]
    key_pos = everything[:, col_width + D_ROPE].astype(jnp.int32) * POS_SPLIT + everything[
        :, col_width + D_ROPE + 1
    ].astype(jnp.int32)

    keys = jnp.dot(comp_all, w_uk, preferred_element_type=jnp.float32).astype(jnp.bfloat16)
    values = jnp.dot(comp_all, w_uv, preferred_element_type=jnp.float32).astype(jnp.bfloat16)
    keys = keys.reshape(key_count, head_count, D_NOPE)
    values = values.reshape(key_count, head_count, D_V)
    queries = q_nope.reshape(row_count, head_count, D_NOPE)
    query_rope = q_rope.reshape(row_count, head_count, D_ROPE)
    grad_out = d_out.reshape(row_count, head_count, D_V)

    scores = jnp.einsum("qhd,khd->hqk", queries, keys, preferred_element_type=jnp.float32)
    scores = scores + jnp.einsum(
        "qhr,kr->hqk", query_rope, rope_all, preferred_element_type=jnp.float32
    )
    scores = scores * soft_scale
    pairs = (key_pos[None, :] <= positions[:, None]) & (
        key_pos[None, :] >= positions[:, None] - spans[:, None]
    )
    masked = jnp.where(pairs[None], scores, lowest)
    row_max = jnp.max(masked, axis=2, keepdims=True)
    row_sum = jnp.sum(
        jnp.where(pairs[None], jnp.exp(masked - row_max), 0.0), axis=2, keepdims=True
    )
    log_norm = row_max + jnp.log(row_sum)
    prob_float = jnp.where(pairs[None], jnp.exp(scores - log_norm), 0.0)
    grad_prob = jnp.einsum("qhd,khd->hqk", grad_out, values, preferred_element_type=jnp.float32)
    delta_rows = jnp.sum(prob_float * grad_prob, axis=2, keepdims=True)
    grad_score = (prob_float * (grad_prob - delta_rows) * soft_scale).astype(jnp.bfloat16)
    prob_half = prob_float.astype(jnp.bfloat16)

    query_grad = jnp.einsum("hqk,khd->qhd", grad_score, keys, preferred_element_type=jnp.float32)
    rope_grad = jnp.einsum("hqk,kr->qhr", grad_score, rope_all, preferred_element_type=jnp.float32)
    stacked_left = jnp.stack([grad_score, prob_half], axis=0)
    stacked_right = jnp.stack(
        [jnp.transpose(queries, (1, 0, 2)), jnp.transpose(grad_out, (1, 0, 2))], axis=0
    )
    both = jnp.einsum(
        "ghqk,ghqd->ghkd", stacked_left, stacked_right, preferred_element_type=jnp.float32
    )
    radices = tuple(d[0] for d in reversed(gather_order(block_count)))
    both = both.reshape(both.shape[:2] + radices + (row_count, both.shape[3]))
    mine = scatter_relative(both, "blk", 2, jnp.bfloat16)
    mine = jnp.transpose(mine, (2, 0, 1, 3)).reshape(row_count, -1)
    flat = mine.astype(jnp.bfloat16)
    key_flat = flat[:, : head_count * D_NOPE]
    value_flat = flat[:, head_count * D_NOPE :]

    def back_project(grad_flat, weight):
        return lax.dot_general(
            grad_flat, weight, (((1,), (1,)), ((), ())), preferred_element_type=jnp.float32
        )

    latent_part = back_project(key_flat, w_uk) + back_project(value_flat, w_uv)
    sum_levels = []
    for radix, stride in digits_of(lax.axis_size("heads")):
        if radix == 4:
            sum_levels += [(2, stride), (2, stride * 2)]
        else:
            sum_levels.append((radix, stride))
    gather_levels = gather_order(block_count)
    comp_own = comp_all.reshape(radices + (row_count, col_width))[0]

    def own_products(flats):
        first_radix, first_stride = gather_levels[0]
        inner = list(reversed(gather_levels[1:-1]))
        slot_sums = []
        for slot in range(first_radix):
            left = comp_own[..., slot, :, :].reshape((-1, row_count, col_width))
            right = flats[..., slot, :, :].reshape((-1, row_count, flat.shape[1]))
            product = jnp.einsum("btl,btk->blk", left, right, preferred_element_type=jnp.float32)
            partial = product.astype(jnp.bfloat16).astype(jnp.float32)
            partial = partial.reshape(tuple(d[0] for d in inner) + partial.shape[1:])
            for radix, stride in inner:
                partial = ordered_sum([partial[k] for k in range(radix)], "blk", radix, stride)
            slot_sums.append(partial)
        return ordered_sum(slot_sums, "blk", first_radix, first_stride)

    latent_sum = latent_part
    flats = flat
    for level in range(max(len(sum_levels), len(gather_levels))):
        if level < len(gather_levels) - 1:
            flats = gather_step(flats, "blk", *gather_levels[level])
        elif level == len(gather_levels) - 1:
            flats = reduce_step(own_products(flats), "blk", *gather_levels[level], jnp.float32)
        if level < len(sum_levels):
            latent_sum = reduce_step(latent_sum, "heads", *sum_levels[level], jnp.bfloat16)
        flats, latent_sum = lax.optimization_barrier((flats, latent_sum))
    grad_latent = (latent_sum * factor).astype(jnp.bfloat16)
    weight_sum = flats
    weight_key_grad = weight_sum[:, : head_count * D_NOPE]
    weight_value_grad = weight_sum[:, head_count * D_NOPE :]

    grad_q_nope = query_grad.reshape(row_count, head_count * D_NOPE).astype(jnp.bfloat16)
    grad_q_rope = rope_grad.reshape(row_count, head_count * D_ROPE).astype(jnp.bfloat16)
    return (grad_q_nope, grad_q_rope, grad_latent, weight_key_grad, weight_value_grad)


def solution(mesh):
    in_specs = (
        P("blk", "heads"),
        P("blk", "heads"),
        P("blk", "heads"),
        P("blk", None),
        P(None, "blk"),
        P("blk"),
        P("blk"),
        P(None, "heads"),
        P(None, "heads"),
    )
    out_specs = (
        P("blk", "heads"),
        P("blk", "heads"),
        P("blk", None),
        P(None, "heads"),
        P(None, "heads"),
    )
    return jax.shard_map(body, mesh=mesh, in_specs=in_specs, out_specs=out_specs, check_vma=False)
```

```python
import jax
import jax.numpy as jnp
from jax import lax
from jax.sharding import PartitionSpec as P

D_ROPE = 64
D_NOPE = 128
D_V = 128
POS_SPLIT = 64
LANE = 128


lowest = -1e30


def digits_of(size):
    found = []
    stride = 1
    rest = size
    for prime in (2, 3):
        if rest % prime == 0:
            found.append((prime, stride))
            stride *= prime
            rest //= prime
    while rest % 4 == 0:
        found.append((4, stride))
        stride *= 4
        rest //= 4
    prime = 2
    while rest > 1:
        while rest % prime == 0:
            found.append((prime, stride))
            stride *= prime
            rest //= prime
        prime += 1
    return found


def gather_order(size):
    return sorted(digits_of(size), key=lambda d: (d[0] != 3, -d[1]))


def digit_value(axis, radix, stride):
    return (lax.axis_index(axis) // stride) % radix


def shift_digit(x, axis, radix, stride, by):
    size = lax.axis_size(axis)
    pairs = []
    for i in range(size):
        r = (i // stride) % radix
        pairs.append((i, i + (((r + by) % radix) - r) * stride))
    return lax.ppermute(x, axis, pairs)


def ordered_pieces(own, axis, radix, stride):
    r = digit_value(axis, radix, stride)
    received = {by: shift_digit(own, axis, radix, stride, by) for by in range(1, radix)}
    return canonical(own, received, r, radix)


def canonical(own, received, r, radix):
    pieces = []
    for k in range(radix):
        piece = own
        for by in range(1, radix):
            piece = jnp.where((r - k) % radix == by, received[by], piece)
        pieces.append(piece)
    return pieces


def gather_step(buf, axis, radix, stride):
    received = [shift_digit(buf, axis, radix, stride, by) for by in range(1, radix)]
    pieces = [buf] + [received[radix - k - 1] for k in range(1, radix)]
    return jnp.stack(pieces, axis=0)


def gather_relative(block, axis):
    buf = block
    levels = gather_order(lax.axis_size(axis))
    for radix, stride in levels[:-1]:
        buf = gather_step(buf, axis, radix, stride)
    width = buf.shape[-1]
    lanes = -(-width // LANE) * LANE
    padded = jnp.pad(buf, [(0, 0)] * (buf.ndim - 1) + [(0, lanes - width)])
    return gather_step(padded, axis, *levels[-1])[..., :width]


def scatter_relative(data, axis, lead, wire):
    for radix, stride in reversed(gather_order(lax.axis_size(axis))):
        head = (slice(None),) * lead
        total = data[head + (0,)]
        for by in range(1, radix):
            part = data[head + (by,)].astype(wire)
            total = total + shift_digit(part, axis, radix, stride, by).astype(jnp.float32)
        data = total
    return data


def ordered_sum(slots, axis, radix, stride):
    r = digit_value(axis, radix, stride)
    received = {by: slots[radix - by] for by in range(1, radix)}
    ordered = canonical(slots[0], received, r, radix)
    total = ordered[0]
    for piece in ordered[1:]:
        total = total + piece
    return total


def reduce_step(x, axis, radix, stride, wire):
    own = x.astype(wire)
    if radix == 2:
        return own.astype(jnp.float32) + shift_digit(own, axis, radix, stride, 1).astype(jnp.float32)
    pieces = ordered_pieces(own, axis, radix, stride)
    total = pieces[0].astype(jnp.float32)
    for piece in pieces[1:]:
        total = total + piece.astype(jnp.float32)
    return total


def body(q_nope, q_rope, d_out, latent, scale_exp, positions, spans, w_uk, w_uv):
    row_count = q_nope.shape[0]
    head_count = w_uk.shape[1] // D_NOPE
    col_width = latent.shape[1] - D_ROPE
    col_group = col_width // scale_exp.shape[0]
    block_count = lax.axis_size("blk")
    key_count = row_count * block_count
    soft_scale = (D_NOPE + D_ROPE) ** (-0.5)

    factor = jnp.exp2(jnp.repeat(jnp.transpose(scale_exp), col_group, axis=1).astype(jnp.float32))
    compressed = (latent[:, :col_width].astype(jnp.float32) * factor).astype(jnp.bfloat16)
    pos_hi = (positions // POS_SPLIT).astype(jnp.bfloat16)
    pos_lo = (positions % POS_SPLIT).astype(jnp.bfloat16)
    packed = jnp.concatenate(
        [compressed, latent[:, col_width:], pos_hi[:, None], pos_lo[:, None]], axis=1
    )
    everything = gather_relative(packed, "blk").reshape(key_count, packed.shape[1])
    comp_all = everything[:, :col_width]
    rope_all = everything[:, col_width : col_width + D_ROPE]
    key_pos = everything[:, col_width + D_ROPE].astype(jnp.int32) * POS_SPLIT + everything[
        :, col_width + D_ROPE + 1
    ].astype(jnp.int32)

    keys = jnp.dot(comp_all, w_uk, preferred_element_type=jnp.float32).astype(jnp.bfloat16)
    values = jnp.dot(comp_all, w_uv, preferred_element_type=jnp.float32).astype(jnp.bfloat16)
    keys = keys.reshape(key_count, head_count, D_NOPE)
    values = values.reshape(key_count, head_count, D_V)
    queries = q_nope.reshape(row_count, head_count, D_NOPE)
    query_rope = q_rope.reshape(row_count, head_count, D_ROPE)
    grad_out = d_out.reshape(row_count, head_count, D_V)

    scores = jnp.einsum("qhd,khd->hqk", queries, keys, preferred_element_type=jnp.float32)
    scores = scores + jnp.einsum(
        "qhr,kr->hqk", query_rope, rope_all, preferred_element_type=jnp.float32
    )
    scores = scores * soft_scale
    pairs = (key_pos[None, :] <= positions[:, None]) & (
        key_pos[None, :] >= positions[:, None] - spans[:, None]
    )
    masked = jnp.where(pairs[None], scores, lowest)
    row_max = jnp.max(masked, axis=2, keepdims=True)
    row_sum = jnp.sum(
        jnp.where(pairs[None], jnp.exp(masked - row_max), 0.0), axis=2, keepdims=True
    )
    log_norm = row_max + jnp.log(row_sum)
    prob_float = jnp.where(pairs[None], jnp.exp(scores - log_norm), 0.0)
    grad_prob = jnp.einsum("qhd,khd->hqk", grad_out, values, preferred_element_type=jnp.float32)
    delta_rows = jnp.sum(prob_float * grad_prob, axis=2, keepdims=True)
    grad_score = (prob_float * (grad_prob - delta_rows) * soft_scale).astype(jnp.bfloat16)
    prob_half = prob_float.astype(jnp.bfloat16)

    query_grad = jnp.einsum("hqk,khd->qhd", grad_score, keys, preferred_element_type=jnp.float32)
    rope_grad = jnp.einsum("hqk,kr->qhr", grad_score, rope_all, preferred_element_type=jnp.float32)
    stacked_left = jnp.stack([grad_score, prob_half], axis=0)
    stacked_right = jnp.stack(
        [jnp.transpose(queries, (1, 0, 2)), jnp.transpose(grad_out, (1, 0, 2))], axis=0
    )
    both = jnp.einsum(
        "ghqk,ghqd->ghkd", stacked_left, stacked_right, preferred_element_type=jnp.float32
    )
    radices = tuple(d[0] for d in reversed(gather_order(block_count)))
    both = both.reshape(both.shape[:2] + radices + (row_count, both.shape[3]))
    mine = scatter_relative(both, "blk", 2, jnp.bfloat16)
    mine = jnp.transpose(mine, (2, 0, 1, 3)).reshape(row_count, -1)
    flat = mine.astype(jnp.bfloat16)
    key_flat = flat[:, : head_count * D_NOPE]
    value_flat = flat[:, head_count * D_NOPE :]

    def back_project(grad_flat, weight):
        return lax.dot_general(
            grad_flat, weight, (((1,), (1,)), ((), ())), preferred_element_type=jnp.float32
        )

    latent_part = back_project(key_flat, w_uk) + back_project(value_flat, w_uv)
    sum_levels = digits_of(lax.axis_size("heads"))
    if len(sum_levels) > 2 and sum_levels[-1][0] == 4:
        last_stride = sum_levels[-1][1]
        sum_levels = sum_levels[:-1] + [(2, last_stride), (2, last_stride * 2)]
    sum_levels = sorted(sum_levels, key=lambda d: -d[0])
    gather_levels = gather_order(block_count)
    comp_own = comp_all.reshape(radices + (row_count, col_width))[0]

    def own_products(flats):
        first_radix, first_stride = gather_levels[0]
        inner = list(reversed(gather_levels[1:-1]))
        slot_sums = []
        for slot in range(first_radix):
            left = comp_own[..., slot, :, :].reshape((-1, row_count, col_width))
            right = flats[..., slot, :, :].reshape((-1, row_count, flat.shape[1]))
            product = jnp.einsum("btl,btk->blk", left, right, preferred_element_type=jnp.float32)
            partial = product.astype(jnp.bfloat16).astype(jnp.float32)
            partial = partial.reshape(tuple(d[0] for d in inner) + partial.shape[1:])
            for radix, stride in inner:
                partial = ordered_sum([partial[k] for k in range(radix)], "blk", radix, stride)
            slot_sums.append(partial)
        return ordered_sum(slot_sums, "blk", first_radix, first_stride)

    latent_sum = latent_part
    flats = flat
    for level in range(max(len(sum_levels), len(gather_levels))):
        if level < len(gather_levels) - 1:
            flats = gather_step(flats, "blk", *gather_levels[level])
        elif level == len(gather_levels) - 1:
            flats = reduce_step(own_products(flats), "blk", *gather_levels[level], jnp.float32)
        if level < len(sum_levels):
            latent_sum = reduce_step(latent_sum, "heads", *sum_levels[level], jnp.bfloat16)
        flats, latent_sum = lax.optimization_barrier((flats, latent_sum))
    grad_latent = (latent_sum * factor).astype(jnp.bfloat16)
    weight_sum = flats
    weight_key_grad = weight_sum[:, : head_count * D_NOPE]
    weight_value_grad = weight_sum[:, head_count * D_NOPE :]

    grad_q_nope = query_grad.reshape(row_count, head_count * D_NOPE).astype(jnp.bfloat16)
    grad_q_rope = rope_grad.reshape(row_count, head_count * D_ROPE).astype(jnp.bfloat16)
    return (grad_q_nope, grad_q_rope, grad_latent, weight_key_grad, weight_value_grad)


def solution(mesh):
    in_specs = (
        P("blk", "heads"),
        P("blk", "heads"),
        P("blk", "heads"),
        P("blk", None),
        P(None, "blk"),
        P("blk"),
        P("blk"),
        P(None, "heads"),
        P(None, "heads"),
    )
    out_specs = (
        P("blk", "heads"),
        P("blk", "heads"),
        P("blk", None),
        P(None, "heads"),
        P(None, "heads"),
    )
    return jax.shard_map(body, mesh=mesh, in_specs=in_specs, out_specs=out_specs, check_vma=False)
```

```python
import jax
import jax.numpy as jnp
from jax import lax
from jax.sharding import PartitionSpec as P

D_ROPE = 64
D_NOPE = 128
D_V = 128
POS_SPLIT = 64
LANE = 128


lowest = -1e30


def digits_of(size):
    found = []
    stride = 1
    rest = size
    for prime in (2, 3):
        if rest % prime == 0:
            found.append((prime, stride))
            stride *= prime
            rest //= prime
    while rest % 4 == 0:
        found.append((4, stride))
        stride *= 4
        rest //= 4
    prime = 2
    while rest > 1:
        while rest % prime == 0:
            found.append((prime, stride))
            stride *= prime
            rest //= prime
        prime += 1
    return found


def gather_order(size):
    return sorted(digits_of(size), key=lambda d: (d[0] != 3, -d[1]))


def digit_value(axis, radix, stride):
    return (lax.axis_index(axis) // stride) % radix


def shift_digit(x, axis, radix, stride, by):
    size = lax.axis_size(axis)
    pairs = []
    for i in range(size):
        r = (i // stride) % radix
        pairs.append((i, i + (((r + by) % radix) - r) * stride))
    return lax.ppermute(x, axis, pairs)


def ordered_pieces(own, axis, radix, stride):
    r = digit_value(axis, radix, stride)
    received = {by: shift_digit(own, axis, radix, stride, by) for by in range(1, radix)}
    return canonical(own, received, r, radix)


def canonical(own, received, r, radix):
    pieces = []
    for k in range(radix):
        piece = own
        for by in range(1, radix):
            piece = jnp.where((r - k) % radix == by, received[by], piece)
        pieces.append(piece)
    return pieces


def gather_step(buf, axis, radix, stride):
    received = [shift_digit(buf, axis, radix, stride, by) for by in range(1, radix)]
    pieces = [buf] + [received[radix - k - 1] for k in range(1, radix)]
    return jnp.stack(pieces, axis=0)


def gather_relative(block, axis):
    buf = block
    levels = gather_order(lax.axis_size(axis))
    for radix, stride in levels[:-1]:
        buf = gather_step(buf, axis, radix, stride)
    width = buf.shape[-1]
    lanes = -(-width // LANE) * LANE
    padded = jnp.pad(buf, [(0, 0)] * (buf.ndim - 1) + [(0, lanes - width)])
    return gather_step(padded, axis, *levels[-1])[..., :width]


def scatter_relative(data, axis, lead, wire):
    for radix, stride in reversed(gather_order(lax.axis_size(axis))):
        head = (slice(None),) * lead
        total = data[head + (0,)]
        for by in range(1, radix):
            part = data[head + (by,)].astype(wire)
            total = total + shift_digit(part, axis, radix, stride, by).astype(jnp.float32)
        data = total
    return data


def ordered_sum(slots, axis, radix, stride):
    r = digit_value(axis, radix, stride)
    received = {by: slots[radix - by] for by in range(1, radix)}
    ordered = canonical(slots[0], received, r, radix)
    total = ordered[0]
    for piece in ordered[1:]:
        total = total + piece
    return total


def reduce_step(x, axis, radix, stride, wire):
    own = x.astype(wire)
    if radix == 2:
        return own.astype(jnp.float32) + shift_digit(own, axis, radix, stride, 1).astype(jnp.float32)
    pieces = ordered_pieces(own, axis, radix, stride)
    total = pieces[0].astype(jnp.float32)
    for piece in pieces[1:]:
        total = total + piece.astype(jnp.float32)
    return total


def body(q_nope, q_rope, d_out, latent, scale_exp, positions, spans, w_uk, w_uv):
    row_count = q_nope.shape[0]
    head_count = w_uk.shape[1] // D_NOPE
    col_width = latent.shape[1] - D_ROPE
    col_group = col_width // scale_exp.shape[0]
    block_count = lax.axis_size("blk")
    key_count = row_count * block_count
    soft_scale = (D_NOPE + D_ROPE) ** (-0.5)

    factor = jnp.exp2(jnp.repeat(jnp.transpose(scale_exp), col_group, axis=1).astype(jnp.float32))
    compressed = (latent[:, :col_width].astype(jnp.float32) * factor).astype(jnp.bfloat16)
    pos_hi = (positions // POS_SPLIT).astype(jnp.bfloat16)
    pos_lo = (positions % POS_SPLIT).astype(jnp.bfloat16)
    packed = jnp.concatenate(
        [compressed, latent[:, col_width:], pos_hi[:, None], pos_lo[:, None]], axis=1
    )
    everything = gather_relative(packed, "blk").reshape(key_count, packed.shape[1])
    comp_all = everything[:, :col_width]
    rope_all = everything[:, col_width : col_width + D_ROPE]
    key_pos = everything[:, col_width + D_ROPE].astype(jnp.int32) * POS_SPLIT + everything[
        :, col_width + D_ROPE + 1
    ].astype(jnp.int32)

    keys = jnp.dot(comp_all, w_uk, preferred_element_type=jnp.float32).astype(jnp.bfloat16)
    values = jnp.dot(comp_all, w_uv, preferred_element_type=jnp.float32).astype(jnp.bfloat16)
    keys = keys.reshape(key_count, head_count, D_NOPE)
    values = values.reshape(key_count, head_count, D_V)
    queries = q_nope.reshape(row_count, head_count, D_NOPE)
    query_rope = q_rope.reshape(row_count, head_count, D_ROPE)
    grad_out = d_out.reshape(row_count, head_count, D_V)

    scores = jnp.einsum("qhd,khd->hqk", queries, keys, preferred_element_type=jnp.float32)
    scores = scores + jnp.einsum(
        "qhr,kr->hqk", query_rope, rope_all, preferred_element_type=jnp.float32
    )
    scores = scores * soft_scale
    pairs = (key_pos[None, :] <= positions[:, None]) & (
        key_pos[None, :] >= positions[:, None] - spans[:, None]
    )
    masked = jnp.where(pairs[None], scores, lowest)
    row_max = jnp.max(masked, axis=2, keepdims=True)
    row_sum = jnp.sum(
        jnp.where(pairs[None], jnp.exp(masked - row_max), 0.0), axis=2, keepdims=True
    )
    log_norm = row_max + jnp.log(row_sum)
    prob_float = jnp.where(pairs[None], jnp.exp(scores - log_norm), 0.0)
    grad_prob = jnp.einsum("qhd,khd->hqk", grad_out, values, preferred_element_type=jnp.float32)
    delta_rows = jnp.sum(prob_float * grad_prob, axis=2, keepdims=True)
    grad_score = (prob_float * (grad_prob - delta_rows) * soft_scale).astype(jnp.bfloat16)
    prob_half = prob_float.astype(jnp.bfloat16)

    query_grad = jnp.einsum("hqk,khd->qhd", grad_score, keys, preferred_element_type=jnp.float32)
    rope_grad = jnp.einsum("hqk,kr->qhr", grad_score, rope_all, preferred_element_type=jnp.float32)
    stacked_left = jnp.stack([grad_score, prob_half], axis=0)
    stacked_right = jnp.stack(
        [jnp.transpose(queries, (1, 0, 2)), jnp.transpose(grad_out, (1, 0, 2))], axis=0
    )
    both = jnp.einsum(
        "ghqk,ghqd->ghkd", stacked_left, stacked_right, preferred_element_type=jnp.float32
    )
    radices = tuple(d[0] for d in reversed(gather_order(block_count)))
    both = both.reshape(both.shape[:2] + radices + (row_count, both.shape[3]))
    mine = scatter_relative(both, "blk", 2, jnp.bfloat16)
    mine = jnp.transpose(mine, (2, 0, 1, 3)).reshape(row_count, -1)
    flat = mine.astype(jnp.bfloat16)
    key_flat = flat[:, : head_count * D_NOPE]
    value_flat = flat[:, head_count * D_NOPE :]

    def back_project(grad_flat, weight):
        return lax.dot_general(
            grad_flat, weight, (((1,), (1,)), ((), ())), preferred_element_type=jnp.float32
        )

    latent_part = back_project(key_flat, w_uk) + back_project(value_flat, w_uv)
    sum_levels = digits_of(lax.axis_size("heads"))
    if len(sum_levels) > 2 and sum_levels[-1][0] == 4:
        last_stride = sum_levels[-1][1]
        sum_levels = sum_levels[:-1] + [(2, last_stride), (2, last_stride * 2)]
    gather_levels = gather_order(block_count)
    comp_own = comp_all.reshape(radices + (row_count, col_width))[0]

    def own_products(flats):
        first_radix, first_stride = gather_levels[0]
        inner = list(reversed(gather_levels[1:-1]))
        slot_sums = []
        for slot in range(first_radix):
            left = comp_own[..., slot, :, :].reshape((-1, row_count, col_width))
            right = flats[..., slot, :, :].reshape((-1, row_count, flat.shape[1]))
            product = jnp.einsum("btl,btk->blk", left, right, preferred_element_type=jnp.float32)
            partial = product.astype(jnp.bfloat16).astype(jnp.float32)
            partial = partial.reshape(tuple(d[0] for d in inner) + partial.shape[1:])
            for radix, stride in inner:
                partial = ordered_sum([partial[k] for k in range(radix)], "blk", radix, stride)
            slot_sums.append(partial)
        return ordered_sum(slot_sums, "blk", first_radix, first_stride)

    latent_sum = latent_part
    flats = flat
    for level in range(max(len(sum_levels), len(gather_levels) + 1)):
        if level < len(gather_levels) - 1:
            flats = gather_step(flats, "blk", *gather_levels[level])
        elif level == len(gather_levels) - 1:
            flats = own_products(flats)
        elif level == len(gather_levels):
            flats = reduce_step(flats, "blk", *gather_levels[-1], jnp.float32)
        if level < len(sum_levels):
            latent_sum = reduce_step(latent_sum, "heads", *sum_levels[level], jnp.bfloat16)
        flats, latent_sum = lax.optimization_barrier((flats, latent_sum))
    grad_latent = (latent_sum * factor).astype(jnp.bfloat16)
    weight_sum = flats
    weight_key_grad = weight_sum[:, : head_count * D_NOPE]
    weight_value_grad = weight_sum[:, head_count * D_NOPE :]

    grad_q_nope = query_grad.reshape(row_count, head_count * D_NOPE).astype(jnp.bfloat16)
    grad_q_rope = rope_grad.reshape(row_count, head_count * D_ROPE).astype(jnp.bfloat16)
    return (grad_q_nope, grad_q_rope, grad_latent, weight_key_grad, weight_value_grad)


def solution(mesh):
    in_specs = (
        P("blk", "heads"),
        P("blk", "heads"),
        P("blk", "heads"),
        P("blk", None),
        P(None, "blk"),
        P("blk"),
        P("blk"),
        P(None, "heads"),
        P(None, "heads"),
    )
    out_specs = (
        P("blk", "heads"),
        P("blk", "heads"),
        P("blk", None),
        P(None, "heads"),
        P(None, "heads"),
    )
    return jax.shard_map(body, mesh=mesh, in_specs=in_specs, out_specs=out_specs, check_vma=False)
```
